32 devices in a mesh: parts: 2 (over y), aux: 4 (over x, core), pair: 4 (over z).
Axes of the slice: x: 2, y: 2, z: 4, core: 2. Of those that a mesh axis runs over, the one named last changes fastest.
Arguments:
- cholesky: bfloat16 [96, 832, 832], P(('parts', 'aux', 'pair')), parts along dimension 0, may hold values from -1.5 to 1.5
- occ_coef: bfloat16 [2, 2, 832, 128], replicated, may hold values from -0.15625 to 0.15625
- vir_coef: bfloat16 [2, 2, 832, 1536], P(None, None, None, 'pair'), may hold values from -0.15625 to 0.15625
- occ_energy: float32 [128], replicated, may hold values from -3 to -0.3
- vir_energy: float32 [1536], replicated, may hold values from 0.2 to 3
- batch_occ: int32 [3], replicated, may hold values from 0 to 127, as said below
Outputs:
- pair_vectors: bfloat16 [96, 128, 2, 1536], P(('parts', 'aux', 'pair')), parts along dimension 0
- amplitudes: float32 [3072, 2, 3, 3, 1536], P(('parts', 'aux'), None, None, None, 'pair'), parts along dimension 0
The draws below stay inside these ranges and needn't reach their ends.
There are 2 independent parts, one for each index of `parts`. The reference program is written for one: setup_inputs(seed, part) draws one part's arguments, and reference() takes and returns one part's arrays. A program takes and returns all parts, laid end to end along the dimension named above; an argument that names none is the same for every part. Nothing has to cross between parts.
Inputs may be any that keep to these rules, and one draw needn't show every extreme that they name: `batch_occ`: 3 distinct occupied indices, the highest occupied spinor 128 - 1 always among them.
All inputs are finite; a program needn't handle non-finite values.
Results may differ from the reference program's by a relative error of at most 0.0064.
Values may be sent and summed in bfloat16 or wider, within the bound.
No kernel may reach another device: no remote copies, remote signals or barrier semaphores. Data moves between devices by JAX's collectives and lax.ppermute only.
A program may use at most 192 MiB of HBM per device.

```python
import jax
import jax.numpy as jnp
from jax import lax

NAO = 832
O = 128
V = 1536
IB = 3
P_SLAB = 48


def draw_batch_occ(key, part):
    first_key = jax.random.fold_in(key, 11)
    second_key = jax.random.fold_in(key, 23)
    others = jax.random.permutation(first_key, O - 1)[:IB - 1].astype(jnp.int32)
    highest = jnp.full((1,), O - 1, jnp.int32)
    joined = jnp.concatenate([others, highest], 0)
    return jax.random.permutation(second_key, joined).astype(jnp.int32)


def level_of(own_key, extent, shards, smallest, largest):
    factor_of = 1.0
    for axis_at, shards_of in shards:
        draws = jax.random.uniform(jax.random.fold_in(jax.random.fold_in(own_key, 6), axis_at), (shards_of,), jnp.float32, smallest / len(shards), largest / len(shards))
        factor_of = factor_of * jnp.repeat(jnp.exp(draws), extent[axis_at] // shards_of).reshape((-1,) + (1,) * (len(extent) - 1 - axis_at))
    return factor_of


def bell_draw(stream_key, extent, scale, most, shards=(), kind=jnp.bfloat16):
    result = scale * jax.random.normal(stream_key, extent, jnp.float32)
    if shards:
        result = result * level_of(stream_key, extent, shards, -0.22, 0.18)
    return jnp.clip(result, -most, most).astype(kind)


def setup_inputs(seed: int = 0, part: int = 0) -> dict:
    arg_keys = jax.random.split(jax.random.key(seed), 7)
    part_keys = jax.random.split(jax.random.fold_in(arg_keys[6], part), 7)
    return {
        "cholesky": bell_draw(part_keys[0], (P_SLAB, NAO, NAO), 0.25, 1.5, ((0, 16),)),
        "occ_coef": bell_draw(arg_keys[1], (2, 2, NAO, O), (2 * NAO) ** -0.5, 0.15625),
        "vir_coef": bell_draw(arg_keys[2], (2, 2, NAO, V), (2 * NAO) ** -0.5, 0.15625, ((3, 4),)),
        "occ_energy": jnp.clip(jax.random.uniform(arg_keys[3], (O,), jnp.float32, -3.0, -0.3), -3.0, -0.3),
        "vir_energy": jnp.clip(jax.random.uniform(arg_keys[4], (V,), jnp.float32, 0.2, 3.0), 0.2, 3.0),
        "batch_occ": draw_batch_occ(jax.random.fold_in(arg_keys[6], 71), part),
    }


def stacked_right(coef_rows):
    middle = coef_rows.shape[0] // 2
    real_rows = coef_rows[:middle]
    imag_rows = coef_rows[middle:]
    real_side = jnp.concatenate([real_rows, -imag_rows], 0)
    imag_side = jnp.concatenate([imag_rows, real_rows], 0)
    return jnp.concatenate([real_side, imag_side], 1)


def pair_terms(batch_rows, column_rows):
    left = jnp.concatenate([batch_rows[:, :, 0, :], batch_rows[:, :, 1, :]], 0).astype(jnp.float32)
    real_right = jnp.concatenate([column_rows[:, :, 0, :], -column_rows[:, :, 1, :]], 0)
    imag_right = jnp.concatenate([column_rows[:, :, 1, :], column_rows[:, :, 0, :]], 0)
    right = jnp.stack([real_right, imag_right], 1).astype(jnp.float32)
    return jnp.einsum('pjb,pcia->bcija', left, right)


def reference(cholesky, occ_coef, vir_coef, occ_energy, vir_energy, batch_occ):
    occ_left = jnp.concatenate([occ_coef[0], -occ_coef[1]], 0).astype(jnp.float32)
    right = stacked_right(vir_coef.reshape(4 * NAO, V))

    def transform(vector):
        half = jnp.einsum('kmj,mn->jkn', occ_left, vector.astype(jnp.float32)).astype(jnp.bfloat16)
        full = jnp.dot(half.reshape(O, 4 * NAO), right, preferred_element_type=jnp.float32).astype(jnp.bfloat16)
        return full.reshape(O, 2, V)

    pair_vectors = lax.map(transform, cholesky)
    selected = jnp.take(pair_vectors, batch_occ, axis=1)
    coulomb = pair_terms(selected, selected)
    paired = coulomb - jnp.swapaxes(coulomb, 2, 3)
    occ_sel = jnp.take(occ_energy, batch_occ)
    denominator = (occ_sel[:, None] + occ_sel[None, :])[None, None, :, :, None] - vir_energy[None, None, None, None, :] - vir_energy[:, None, None, None, None]
    amplitudes = paired / denominator
    return (pair_vectors, amplitudes)
```

```python
import jax
import jax.numpy as jnp
from jax import lax
from jax.sharding import PartitionSpec as P


def complex_rows(half):
    real_part, imag_part = half[..., :2, :], half[..., 2:, :]
    c0 = jnp.concatenate([real_part, -imag_part], -2)
    c1 = jnp.concatenate([imag_part, real_part], -2)
    return jnp.stack([c0, c1], -3)


def pair_terms(batch_rows, column_rows):
    left = jnp.concatenate([batch_rows[:, :, 0, :], batch_rows[:, :, 1, :]], 0)
    real_right = jnp.concatenate([column_rows[:, :, 0, :], -column_rows[:, :, 1, :]], 0)
    imag_right = jnp.concatenate([column_rows[:, :, 1, :], column_rows[:, :, 0, :]], 0)
    right = jnp.stack([real_right, imag_right], 1)
    return jnp.einsum("pjb,pcia->bcija", left, right, preferred_element_type=jnp.float32)


def on_device(cholesky, occ_coef, vir_coef, occ_energy, vir_energy, batch_occ):
    vectors = cholesky.shape[0]
    orbitals = cholesky.shape[1]
    occupied = occ_coef.shape[3]
    a_width = vir_coef.shape[3]
    n_pair = lax.axis_size("pair")
    n_aux = lax.axis_size("aux")
    n_parts = lax.axis_size("parts")
    rows = 4 * orbitals
    virtuals = n_pair * a_width

    occ_left = jnp.concatenate([occ_coef[0], -occ_coef[1]], 0)
    v_local = vir_coef.reshape(rows, a_width)

    occ_sel = jnp.take(occ_left, batch_occ, axis=2)
    half_sel = jnp.einsum(
        "kmi,pmn->pikn", occ_sel, cholesky, preferred_element_type=jnp.float32
    ).astype(jnp.bfloat16)
    half_sel_all = lax.all_gather(half_sel, ("aux", "pair"), axis=0, tiled=True)
    count = half_sel_all.shape[0]
    batch = half_sel_all.shape[1]
    lhs_sel = complex_rows(half_sel_all).reshape(count * batch * 2, rows)
    sel_own = jnp.dot(lhs_sel, v_local, preferred_element_type=jnp.float32).astype(jnp.bfloat16)
    sel_own = sel_own.reshape(count, batch, 2, a_width)

    n_q = n_parts * n_aux
    rows_q = rows // n_q
    q = lax.axis_index("parts") * n_aux + lax.axis_index("aux")
    piece = lax.dynamic_slice_in_dim(v_local, q * rows_q, rows_q, 0)
    stage1 = lax.all_gather(piece, "pair", axis=0)
    stage2 = lax.all_gather(stage1, ("parts", "aux"), axis=1)
    v_full = stage2.reshape(n_pair, rows, a_width)

    half = jnp.einsum(
        "kmj,pmn->pjkn", occ_left, cholesky, preferred_element_type=jnp.float32
    ).astype(jnp.bfloat16)
    lhs = complex_rows(half).reshape(vectors * occupied * 2, rows)
    full = jnp.einsum("mk,bkn->mbn", lhs, v_full, preferred_element_type=jnp.float32)
    pair_vectors = full.astype(jnp.bfloat16).reshape(vectors, occupied, 2, virtuals)

    a_start = lax.axis_index("pair") * a_width
    b_width = virtuals // n_aux
    b_start = lax.axis_index("aux") * b_width
    sel_full = lax.all_gather(sel_own, "pair", axis=3, tiled=True)
    sel_b = lax.dynamic_slice_in_dim(sel_full, b_start, b_width, 3)
    coulomb = pair_terms(sel_b, sel_own)
    paired = coulomb - jnp.swapaxes(coulomb, 2, 3)
    occ_e = jnp.take(occ_energy, batch_occ)
    vir_first = lax.dynamic_slice_in_dim(vir_energy, a_start, a_width)
    vir_second = lax.dynamic_slice_in_dim(vir_energy, b_start, b_width)
    denominator = (
        (occ_e[:, None] + occ_e[None, :])[None, None, :, :, None]
        - vir_first[None, None, None, None, :]
        - vir_second[:, None, None, None, None]
    )
    return (pair_vectors, paired / denominator)


def solution(mesh):
    return jax.shard_map(
        on_device,
        mesh=mesh,
        in_specs=(
            P(("parts", "aux", "pair"), None, None),
            P(),
            P(None, None, None, "pair"),
            P(),
            P(),
            P(),
        ),
        out_specs=(
            P(("parts", "aux", "pair"), None, None, None),
            P(("parts", "aux"), None, None, None, "pair"),
        ),
        check_vma=False,
    )
```

```python
import functools

import jax
import jax.numpy as jnp
from jax import lax
from jax.experimental import pallas as pl
from jax.experimental.pallas import tpu as pltpu
from jax.sharding import PartitionSpec as P


def transform_kernel(orbitals, h_ref, v_ref, o_ref):
    real = None
    imag = None
    for s in range(2):
        hr = h_ref[0, s]
        hi = h_ref[0, 2 + s]
        vr = v_ref[0, s * orbitals:(s + 1) * orbitals, :]
        vi = v_ref[0, (2 + s) * orbitals:(3 + s) * orbitals, :]
        rr = jnp.dot(hr, vr, preferred_element_type=jnp.float32)
        ii = jnp.dot(hi, vi, preferred_element_type=jnp.float32)
        ri = jnp.dot(hr, vi, preferred_element_type=jnp.float32)
        ir = jnp.dot(hi, vr, preferred_element_type=jnp.float32)
        real = rr - ii if real is None else real + rr - ii
        imag = ri + ir if imag is None else imag + ri + ir
    o_ref[0, 0] = real.astype(o_ref.dtype)
    o_ref[0, 1] = imag.astype(o_ref.dtype)


def transform(half, v_blocks):
    pn, _, m, n = half.shape
    b, rows, w = v_blocks.shape
    if w % 128 != 0:
        v = v_blocks.reshape(b, 2, 2, n, w)
        hr, hi = half[:, :2], half[:, 2:]
        dims = "pskn,bsnw->pkbw"
        real = jnp.einsum(dims, hr, v[:, 0], preferred_element_type=jnp.float32) - jnp.einsum(
            dims, hi, v[:, 1], preferred_element_type=jnp.float32)
        imag = jnp.einsum(dims, hr, v[:, 1], preferred_element_type=jnp.float32) + jnp.einsum(
            dims, hi, v[:, 0], preferred_element_type=jnp.float32)
        out = jnp.stack([real, imag], 1).astype(jnp.bfloat16)
        return out.reshape(pn, 2, m, b * w)
    flops = 16 * pn * m * n * w * b
    bytes_accessed = 2 * (half.size * b + v_blocks.size + pn * 2 * m * b * w)
    return pl.pallas_call(
        functools.partial(transform_kernel, n),
        grid=(b, pn),
        in_specs=[
            pl.BlockSpec((1, 4, m, n), lambda i, p: (p, 0, 0, 0)),
            pl.BlockSpec((1, rows, w), lambda i, p: (i, 0, 0)),
        ],
        out_specs=pl.BlockSpec((1, 2, m, w), lambda i, p: (p, 0, 0, i)),
        out_shape=jax.ShapeDtypeStruct((pn, 2, m, b * w), jnp.bfloat16),
        cost_estimate=pl.CostEstimate(flops=flops, bytes_accessed=bytes_accessed, transcendentals=0),
    )(half, v_blocks)


def on_device(cholesky, occ_coef, vir_coef, occ_energy, vir_energy, batch_occ):
    vectors = cholesky.shape[0]
    orbitals = cholesky.shape[1]
    occupied = occ_coef.shape[3]
    a_width = vir_coef.shape[3]
    n_pair = lax.axis_size("pair")
    n_aux = lax.axis_size("aux")
    n_parts = lax.axis_size("parts")
    rows = 4 * orbitals
    virtuals = n_pair * a_width
    b_width = virtuals // n_aux
    per_b = b_width // a_width
    batch = batch_occ.shape[0]

    occ_left = jnp.concatenate([occ_coef[0], -occ_coef[1]], 0)
    v_local = vir_coef.reshape(rows, a_width)

    occ_sel = jnp.take(occ_left, batch_occ, axis=2)
    half_sel = jnp.einsum(
        "kmi,pmn->pikn", occ_sel, cholesky, preferred_element_type=jnp.float32
    ).astype(jnp.bfloat16)
    half_sel = half_sel.reshape(vectors * batch * 4, orbitals)
    gathered = lax.all_gather(half_sel, ("aux", "pair"), axis=0)
    count = gathered.shape[0] * vectors
    half_rows = gathered.reshape(count * batch, 4, orbitals).transpose(1, 0, 2)
    sel_own = transform(half_rows[None], v_local[None])
    sel_own = sel_own.reshape(2, count, batch, a_width)

    n_q = n_parts * n_aux
    rows_q = rows // n_q
    q = lax.axis_index("parts") * n_aux + lax.axis_index("aux")
    piece = lax.dynamic_slice_in_dim(v_local, q * rows_q, rows_q, 0)
    stage1 = lax.all_gather(piece, "pair", axis=0)
    stage2 = lax.all_gather(stage1, ("parts", "aux"), axis=1)
    v_full = stage2.reshape(n_pair, rows, a_width)

    half = jnp.einsum(
        "kmj,pmn->pkjn", occ_left, cholesky, preferred_element_type=jnp.float32
    ).astype(jnp.bfloat16)
    full = transform(half, v_full)
    pair_vectors = full.transpose(0, 2, 1, 3)

    sel_all = lax.all_gather(sel_own, "pair", axis=0)
    sel_b = lax.dynamic_slice_in_dim(sel_all, lax.axis_index("aux") * per_b, per_b, 0)
    sel_b = sel_b.transpose(1, 2, 3, 0, 4).reshape(2 * count, batch, b_width)
    left = sel_b.reshape(2 * count * batch, b_width)
    real_right = jnp.concatenate([sel_own[0], -sel_own[1]], 0)
    imag_right = jnp.concatenate([sel_own[1], sel_own[0]], 0)
    right = jnp.stack([real_right, imag_right], 2)
    eye = jnp.arange(batch)[:, None] == jnp.arange(batch)[None, :]
    first = jnp.where(eye[None, :, None, :, None, None], right[:, None, :, None, :, :], 0)
    second = jnp.where(eye[None, :, :, None, None, None], right[:, None, None, :, :, :], 0)
    stacked = (first - second).reshape(2 * count * batch, batch * batch * 2 * a_width)
    paired = lax.dot_general(
        left, stacked, (((0,), (0,)), ((), ())), preferred_element_type=jnp.float32
    ).reshape(b_width, batch, batch, 2, a_width)

    a_start = lax.axis_index("pair") * a_width
    b_start = lax.axis_index("aux") * b_width
    occ_e = jnp.take(occ_energy, batch_occ)
    vir_first = lax.dynamic_slice_in_dim(vir_energy, a_start, a_width)
    vir_second = lax.dynamic_slice_in_dim(vir_energy, b_start, b_width)
    denominator = (
        (occ_e[:, None] + occ_e[None, :])[None, :, :, None, None]
        - vir_first[None, None, None, None, :]
        - vir_second[:, None, None, None, None]
    )
    amplitudes = (paired / denominator).transpose(0, 3, 1, 2, 4)
    return (pair_vectors, amplitudes)


def solution(mesh):
    return jax.shard_map(
        on_device,
        mesh=mesh,
        in_specs=(
            P(("parts", "aux", "pair"), None, None),
            P(),
            P(None, None, None, "pair"),
            P(),
            P(),
            P(),
        ),
        out_specs=(
            P(("parts", "aux", "pair"), None, None, None),
            P(("parts", "aux"), None, None, None, "pair"),
        ),
        check_vma=False,
    )
```

```python
import functools

import jax
import jax.numpy as jnp
from jax import lax
from jax.experimental import pallas as pl
from jax.experimental.pallas import tpu as pltpu
from jax.sharding import PartitionSpec as P


def transform_kernel(orbitals, h_ref, v_ref, o_ref):
    pn, _, m, n = h_ref.shape
    real = None
    imag = None
    for s in range(2):
        hr = h_ref[:, s].reshape(pn * m, n)
        hi = h_ref[:, 2 + s].reshape(pn * m, n)
        vr = v_ref[0, s * orbitals:(s + 1) * orbitals, :]
        vi = v_ref[0, (2 + s) * orbitals:(3 + s) * orbitals, :]
        rr = jnp.dot(hr, vr, preferred_element_type=jnp.float32)
        ii = jnp.dot(hi, vi, preferred_element_type=jnp.float32)
        ri = jnp.dot(hr, vi, preferred_element_type=jnp.float32)
        ir = jnp.dot(hi, vr, preferred_element_type=jnp.float32)
        real = rr - ii if real is None else real + rr - ii
        imag = ri + ir if imag is None else imag + ri + ir
    w = real.shape[1]
    o_ref[:, 0] = real.reshape(pn, m, w).astype(o_ref.dtype)
    o_ref[:, 1] = imag.reshape(pn, m, w).astype(o_ref.dtype)


def transform(half, v_blocks):
    pn, _, m, n = half.shape
    b, rows, w = v_blocks.shape
    if w % 128 != 0:
        v = v_blocks.reshape(b, 2, 2, n, w)
        hr, hi = half[:, :2], half[:, 2:]
        dims = "pskn,bsnw->pkbw"
        real = jnp.einsum(dims, hr, v[:, 0], preferred_element_type=jnp.float32) - jnp.einsum(
            dims, hi, v[:, 1], preferred_element_type=jnp.float32)
        imag = jnp.einsum(dims, hr, v[:, 1], preferred_element_type=jnp.float32) + jnp.einsum(
            dims, hi, v[:, 0], preferred_element_type=jnp.float32)
        out = jnp.stack([real, imag], 1).astype(jnp.bfloat16)
        return out.reshape(pn, 2, m, b * w)
    flops = 16 * pn * m * n * w * b
    bytes_accessed = 2 * (half.size + v_blocks.size + pn * 2 * m * b * w)
    return pl.pallas_call(
        functools.partial(transform_kernel, n),
        grid=(b,),
        in_specs=[
            pl.BlockSpec((pn, 4, m, n), lambda i: (0, 0, 0, 0)),
            pl.BlockSpec((1, rows, w), lambda i: (i, 0, 0)),
        ],
        out_specs=pl.BlockSpec((pn, 2, m, w), lambda i: (0, 0, 0, i)),
        out_shape=jax.ShapeDtypeStruct((pn, 2, m, b * w), jnp.bfloat16),
        cost_estimate=pl.CostEstimate(flops=flops, bytes_accessed=bytes_accessed, transcendentals=0),
    )(half, v_blocks)


def pair_terms(batch_rows, column_rows):
    left = jnp.concatenate([batch_rows[:, :, 0, :], batch_rows[:, :, 1, :]], 0)
    real_right = jnp.concatenate([column_rows[:, :, 0, :], -column_rows[:, :, 1, :]], 0)
    imag_right = jnp.concatenate([column_rows[:, :, 1, :], column_rows[:, :, 0, :]], 0)
    right = jnp.stack([real_right, imag_right], 1)
    return jnp.einsum("pjb,pcia->bcija", left, right, preferred_element_type=jnp.float32)


def gather_group(x, axes, sizes):
    n = 1
    for size in sizes:
        n *= size
    if n > 16:
        return lax.all_gather(x, axes, axis=0)
    me = lax.axis_index(axes[0])
    for name, size in zip(axes[1:], sizes[1:]):
        me = me * size + lax.axis_index(name)
    blocks = [x]
    for shift in range(1, n):
        perm = [(i, (i + shift) % n) for i in range(n)]
        blocks.append(lax.ppermute(x, axes, perm))
    stacked = jnp.stack(blocks, 0)
    return jnp.take(stacked, (me - jnp.arange(n)) % n, axis=0)


def on_device(cholesky, occ_coef, vir_coef, occ_energy, vir_energy, batch_occ):
    vectors = cholesky.shape[0]
    orbitals = cholesky.shape[1]
    occupied = occ_coef.shape[3]
    a_width = vir_coef.shape[3]
    n_pair = lax.axis_size("pair")
    n_aux = lax.axis_size("aux")
    n_parts = lax.axis_size("parts")
    rows = 4 * orbitals
    virtuals = n_pair * a_width
    b_width = virtuals // n_aux
    per_b = b_width // a_width
    batch = batch_occ.shape[0]

    occ_left = jnp.concatenate([occ_coef[0], -occ_coef[1]], 0)
    v_local = vir_coef.reshape(rows, a_width)

    occ_sel = jnp.take(occ_left, batch_occ, axis=2)
    half_sel = jnp.einsum(
        "kmi,pmn->pikn", occ_sel, cholesky, preferred_element_type=jnp.float32
    ).astype(jnp.bfloat16)
    half_sel = half_sel.reshape(vectors * batch * 4, orbitals)
    gathered = gather_group(half_sel, ("aux", "pair"), (n_aux, n_pair))
    count = gathered.shape[0] * vectors
    half_rows = gathered.reshape(count * batch, 4, orbitals).transpose(1, 0, 2)
    sel_own = transform(half_rows[None], v_local[None])
    sel_own = sel_own.reshape(2, count, batch, a_width)

    n_q = n_parts * n_aux
    rows_q = rows // n_q
    q = lax.axis_index("parts") * n_aux + lax.axis_index("aux")
    piece = lax.dynamic_slice_in_dim(v_local, q * rows_q, rows_q, 0)
    stage1 = lax.all_gather(piece, "pair", axis=0)
    half = jnp.einsum(
        "kmj,pmn->pkjn", occ_left, cholesky, preferred_element_type=jnp.float32
    ).astype(jnp.bfloat16)
    stage1, half = lax.optimization_barrier((stage1, half))
    stage2 = lax.all_gather(stage1, ("parts", "aux"), axis=1)
    v_full = stage2.reshape(n_pair, rows, a_width)
    full = transform(half, v_full)
    pair_vectors = full.transpose(0, 2, 1, 3)

    sel_a = sel_own.transpose(1, 2, 0, 3)
    if n_aux == n_pair:
        perm = [(a * n_pair + z, z * n_pair + a) for a in range(n_aux) for z in range(n_pair)]
        sel_b = lax.ppermute(sel_a, ("aux", "pair"), perm)
    else:
        sel_all = lax.all_gather(sel_a, "pair", axis=0)
        sel_b = lax.dynamic_slice_in_dim(sel_all, lax.axis_index("aux") * per_b, per_b, 0)
        sel_b = sel_b.transpose(1, 2, 3, 0, 4).reshape(count, batch, 2, b_width)
    coulomb = pair_terms(sel_b, sel_a)
    paired = coulomb - jnp.swapaxes(coulomb, 2, 3)

    a_start = lax.axis_index("pair") * a_width
    b_start = lax.axis_index("aux") * b_width
    occ_e = jnp.take(occ_energy, batch_occ)
    vir_first = lax.dynamic_slice_in_dim(vir_energy, a_start, a_width)
    vir_second = lax.dynamic_slice_in_dim(vir_energy, b_start, b_width)
    denominator = (
        (occ_e[:, None] + occ_e[None, :])[None, None, :, :, None]
        - vir_first[None, None, None, None, :]
        - vir_second[:, None, None, None, None]
    )
    amplitudes = paired / denominator
    return (pair_vectors, amplitudes)


def solution(mesh):
    return jax.shard_map(
        on_device,
        mesh=mesh,
        in_specs=(
            P(("parts", "aux", "pair"), None, None),
            P(),
            P(None, None, None, "pair"),
            P(),
            P(),
            P(),
        ),
        out_specs=(
            P(("parts", "aux", "pair"), None, None, None),
            P(("parts", "aux"), None, None, None, "pair"),
        ),
        check_vma=False,
    )
```

```python
import functools

import jax
import jax.numpy as jnp
from jax import lax
from jax.experimental import pallas as pl
from jax.experimental.pallas import tpu as pltpu
from jax.sharding import PartitionSpec as P


def transform_kernel(orbitals, h_ref, v_ref, o_ref):
    pn, _, m, n = h_ref.shape
    real = None
    imag = None
    for s in range(2):
        hr = h_ref[:, s].reshape(pn * m, n)
        hi = h_ref[:, 2 + s].reshape(pn * m, n)
        vr = v_ref[0, s * orbitals:(s + 1) * orbitals, :]
        vi = v_ref[0, (2 + s) * orbitals:(3 + s) * orbitals, :]
        rr = jnp.dot(hr, vr, preferred_element_type=jnp.float32)
        ii = jnp.dot(hi, vi, preferred_element_type=jnp.float32)
        ri = jnp.dot(hr, vi, preferred_element_type=jnp.float32)
        ir = jnp.dot(hi, vr, preferred_element_type=jnp.float32)
        real = rr - ii if real is None else real + rr - ii
        imag = ri + ir if imag is None else imag + ri + ir
    w = real.shape[1]
    o_ref[:, 0] = real.reshape(pn, m, w).astype(o_ref.dtype)
    o_ref[:, 1] = imag.reshape(pn, m, w).astype(o_ref.dtype)


def transform(half, v_blocks):
    pn, _, m, n = half.shape
    b, rows, w = v_blocks.shape
    if w % 128 != 0:
        v = v_blocks.reshape(b, 2, 2, n, w)
        hr, hi = half[:, :2], half[:, 2:]
        dims = "pskn,bsnw->pkbw"
        real = jnp.einsum(dims, hr, v[:, 0], preferred_element_type=jnp.float32) - jnp.einsum(
            dims, hi, v[:, 1], preferred_element_type=jnp.float32)
        imag = jnp.einsum(dims, hr, v[:, 1], preferred_element_type=jnp.float32) + jnp.einsum(
            dims, hi, v[:, 0], preferred_element_type=jnp.float32)
        out = jnp.stack([real, imag], 1).astype(jnp.bfloat16)
        return out.reshape(pn, 2, m, b * w)
    flops = 16 * pn * m * n * w * b
    bytes_accessed = 2 * (half.size + v_blocks.size + pn * 2 * m * b * w)
    return pl.pallas_call(
        functools.partial(transform_kernel, n),
        grid=(b,),
        in_specs=[
            pl.BlockSpec((pn, 4, m, n), lambda i: (0, 0, 0, 0)),
            pl.BlockSpec((1, rows, w), lambda i: (i, 0, 0)),
        ],
        out_specs=pl.BlockSpec((pn, 2, m, w), lambda i: (0, 0, 0, i)),
        out_shape=jax.ShapeDtypeStruct((pn, 2, m, b * w), jnp.bfloat16),
        cost_estimate=pl.CostEstimate(flops=flops, bytes_accessed=bytes_accessed, transcendentals=0),
    )(half, v_blocks)


def pair_terms(batch_rows, column_rows):
    left = jnp.concatenate([batch_rows[:, :, 0, :], batch_rows[:, :, 1, :]], 0)
    real_right = jnp.concatenate([column_rows[:, :, 0, :], -column_rows[:, :, 1, :]], 0)
    imag_right = jnp.concatenate([column_rows[:, :, 1, :], column_rows[:, :, 0, :]], 0)
    right = jnp.stack([real_right, imag_right], 1)
    return jnp.einsum("pjb,pcia->bcija", left, right, preferred_element_type=jnp.float32)


def gather_group(x, axes, sizes):
    n = 1
    for size in sizes:
        n *= size
    if n > 16:
        return lax.all_gather(x, axes, axis=0)
    me = lax.axis_index(axes[0])
    for name, size in zip(axes[1:], sizes[1:]):
        me = me * size + lax.axis_index(name)
    blocks = [x]
    for shift in range(1, n):
        perm = [(i, (i + shift) % n) for i in range(n)]
        blocks.append(lax.ppermute(x, axes, perm))
    stacked = jnp.stack(blocks, 0)
    return jnp.take(stacked, (me - jnp.arange(n)) % n, axis=0)


def on_device(cholesky, occ_coef, vir_coef, occ_energy, vir_energy, batch_occ):
    vectors = cholesky.shape[0]
    orbitals = cholesky.shape[1]
    occupied = occ_coef.shape[3]
    a_width = vir_coef.shape[3]
    n_pair = lax.axis_size("pair")
    n_aux = lax.axis_size("aux")
    n_parts = lax.axis_size("parts")
    rows = 4 * orbitals
    virtuals = n_pair * a_width
    b_width = virtuals // n_aux
    per_b = b_width // a_width
    batch = batch_occ.shape[0]

    occ_left = jnp.concatenate([occ_coef[0], -occ_coef[1]], 0)
    v_local = vir_coef.reshape(rows, a_width)

    occ_sel = jnp.take(occ_left, batch_occ, axis=2)
    half_sel = jnp.einsum(
        "kmi,pmn->pikn", occ_sel, cholesky, preferred_element_type=jnp.float32
    ).astype(jnp.bfloat16)
    sel_size = half_sel.size
    sel_rows = -(-sel_size // a_width)
    sel_flat = jnp.pad(half_sel.reshape(-1), (0, sel_rows * a_width - sel_size))

    n_q = n_parts * n_aux
    rows_q = rows // n_q
    me_pair = lax.axis_index("pair")
    q = lax.axis_index("parts") * n_aux + lax.axis_index("aux")
    piece = lax.dynamic_slice_in_dim(v_local, q * rows_q, rows_q, 0)
    carried = jnp.concatenate([piece, sel_flat.reshape(sel_rows, a_width)], 0)
    stage1 = lax.all_gather(carried, "pair", axis=0)

    half = jnp.einsum(
        "kmj,pmn->pkjn", occ_left, cholesky, preferred_element_type=jnp.float32
    ).astype(jnp.bfloat16)
    own = transform(half, v_local[None]).transpose(0, 2, 1, 3)
    stage1, half, own = lax.optimization_barrier((stage1, half, own))
    pair_vectors = jnp.zeros((vectors, occupied, 2, virtuals), jnp.bfloat16)
    pair_vectors = lax.dynamic_update_slice_in_dim(pair_vectors, own, me_pair * a_width, 3)

    sel_pair = stage1[:, rows_q:].reshape(n_pair, -1)[:, :sel_size]
    gathered = gather_group(sel_pair, ("aux",), (n_aux,))
    count = n_aux * n_pair * vectors
    half_rows = gathered.reshape(count * batch, 4, orbitals).transpose(1, 0, 2)
    sel_own = transform(half_rows[None], v_local[None])
    sel_own = sel_own.reshape(2, count, batch, a_width)

    pieces = stage1[:, :rows_q]
    for step in range(1, n_pair):
        block = (me_pair + step) % n_pair
        part = lax.dynamic_index_in_dim(pieces, block, 0, keepdims=False)
        v_block = lax.all_gather(part, ("parts", "aux"), axis=0, tiled=True)
        done = transform(half, v_block[None]).transpose(0, 2, 1, 3)
        pair_vectors = lax.dynamic_update_slice_in_dim(pair_vectors, done, block * a_width, 3)

    sel_a = sel_own.transpose(1, 2, 0, 3)
    if n_aux == n_pair:
        perm = [(a * n_pair + z, z * n_pair + a) for a in range(n_aux) for z in range(n_pair)]
        sel_b = lax.ppermute(sel_a, ("aux", "pair"), perm)
    else:
        sel_all = lax.all_gather(sel_a, "pair", axis=0)
        sel_b = lax.dynamic_slice_in_dim(sel_all, lax.axis_index("aux") * per_b, per_b, 0)
        sel_b = sel_b.transpose(1, 2, 3, 0, 4).reshape(count, batch, 2, b_width)
    coulomb = pair_terms(sel_b, sel_a)
    paired = coulomb - jnp.swapaxes(coulomb, 2, 3)

    a_start = lax.axis_index("pair") * a_width
    b_start = lax.axis_index("aux") * b_width
    occ_e = jnp.take(occ_energy, batch_occ)
    vir_first = lax.dynamic_slice_in_dim(vir_energy, a_start, a_width)
    vir_second = lax.dynamic_slice_in_dim(vir_energy, b_start, b_width)
    denominator = (
        (occ_e[:, None] + occ_e[None, :])[None, None, :, :, None]
        - vir_first[None, None, None, None, :]
        - vir_second[:, None, None, None, None]
    )
    amplitudes = paired / denominator
    return (pair_vectors, amplitudes)


def solution(mesh):
    return jax.shard_map(
        on_device,
        mesh=mesh,
        in_specs=(
            P(("parts", "aux", "pair"), None, None),
            P(),
            P(None, None, None, "pair"),
            P(),
            P(),
            P(),
        ),
        out_specs=(
            P(("parts", "aux", "pair"), None, None, None),
            P(("parts", "aux"), None, None, None, "pair"),
        ),
        check_vma=False,
    )
```

```python
import functools

import jax
import jax.numpy as jnp
from jax import lax
from jax.experimental import pallas as pl
from jax.experimental.pallas import tpu as pltpu
from jax.sharding import PartitionSpec as P


def transform_kernel(orbitals, h_ref, v_ref, o_ref):
    pn, _, m, n = h_ref.shape
    real = None
    imag = None
    for s in range(2):
        hr = h_ref[:, s].reshape(pn * m, n)
        hi = h_ref[:, 2 + s].reshape(pn * m, n)
        vr = v_ref[0, s * orbitals:(s + 1) * orbitals, :]
        vi = v_ref[0, (2 + s) * orbitals:(3 + s) * orbitals, :]
        rr = jnp.dot(hr, vr, preferred_element_type=jnp.float32)
        ii = jnp.dot(hi, vi, preferred_element_type=jnp.float32)
        ri = jnp.dot(hr, vi, preferred_element_type=jnp.float32)
        ir = jnp.dot(hi, vr, preferred_element_type=jnp.float32)
        real = rr - ii if real is None else real + rr - ii
        imag = ri + ir if imag is None else imag + ri + ir
    w = real.shape[1]
    o_ref[:, 0] = real.reshape(pn, m, w).astype(o_ref.dtype)
    o_ref[:, 1] = imag.reshape(pn, m, w).astype(o_ref.dtype)


def transform(half, v_blocks):
    pn, _, m, n = half.shape
    b, rows, w = v_blocks.shape
    if w % 128 != 0:
        v = v_blocks.reshape(b, 2, 2, n, w)
        hr, hi = half[:, :2], half[:, 2:]
        dims = "pskn,bsnw->pkbw"
        real = jnp.einsum(dims, hr, v[:, 0], preferred_element_type=jnp.float32) - jnp.einsum(
            dims, hi, v[:, 1], preferred_element_type=jnp.float32)
        imag = jnp.einsum(dims, hr, v[:, 1], preferred_element_type=jnp.float32) + jnp.einsum(
            dims, hi, v[:, 0], preferred_element_type=jnp.float32)
        out = jnp.stack([real, imag], 1).astype(jnp.bfloat16)
        return out.reshape(pn, 2, m, b * w)
    flops = 16 * pn * m * n * w * b
    bytes_accessed = 2 * (half.size + v_blocks.size + pn * 2 * m * b * w)
    return pl.pallas_call(
        functools.partial(transform_kernel, n),
        grid=(b,),
        in_specs=[
            pl.BlockSpec((pn, 4, m, n), lambda i: (0, 0, 0, 0)),
            pl.BlockSpec((1, rows, w), lambda i: (i, 0, 0)),
        ],
        out_specs=pl.BlockSpec((pn, 2, m, w), lambda i: (0, 0, 0, i)),
        out_shape=jax.ShapeDtypeStruct((pn, 2, m, b * w), jnp.bfloat16),
        cost_estimate=pl.CostEstimate(flops=flops, bytes_accessed=bytes_accessed, transcendentals=0),
    )(half, v_blocks)


def pair_terms(batch_rows, column_rows):
    left = jnp.concatenate([batch_rows[:, :, 0, :], batch_rows[:, :, 1, :]], 0)
    real_right = jnp.concatenate([column_rows[:, :, 0, :], -column_rows[:, :, 1, :]], 0)
    imag_right = jnp.concatenate([column_rows[:, :, 1, :], column_rows[:, :, 0, :]], 0)
    right = jnp.stack([real_right, imag_right], 1)
    return jnp.einsum("pjb,pcia->bcija", left, right, preferred_element_type=jnp.float32)


def gather_group(x, axes, sizes):
    n = 1
    for size in sizes:
        n *= size
    if n > 16:
        return lax.all_gather(x, axes, axis=0)
    me = lax.axis_index(axes[0])
    for name, size in zip(axes[1:], sizes[1:]):
        me = me * size + lax.axis_index(name)
    blocks = [x]
    for shift in range(1, n):
        perm = [(i, (i + shift) % n) for i in range(n)]
        blocks.append(lax.ppermute(x, axes, perm))
    stacked = jnp.stack(blocks, 0)
    return jnp.take(stacked, (me - jnp.arange(n)) % n, axis=0)


def on_device(cholesky, occ_coef, vir_coef, occ_energy, vir_energy, batch_occ):
    vectors = cholesky.shape[0]
    orbitals = cholesky.shape[1]
    occupied = occ_coef.shape[3]
    a_width = vir_coef.shape[3]
    n_pair = lax.axis_size("pair")
    n_aux = lax.axis_size("aux")
    n_parts = lax.axis_size("parts")
    rows = 4 * orbitals
    virtuals = n_pair * a_width
    b_width = virtuals // n_aux
    per_b = b_width // a_width
    batch = batch_occ.shape[0]

    occ_left = jnp.concatenate([occ_coef[0], -occ_coef[1]], 0)
    v_local = vir_coef.reshape(rows, a_width)

    occ_sel = jnp.take(occ_left, batch_occ, axis=2)
    half_sel = jnp.einsum(
        "kmi,pmn->pikn", occ_sel, cholesky, preferred_element_type=jnp.float32
    ).astype(jnp.bfloat16)
    sel_size = half_sel.size
    sel_rows = -(-sel_size // a_width)
    sel_flat = jnp.pad(half_sel.reshape(-1), (0, sel_rows * a_width - sel_size))

    n_q = n_parts * n_aux
    rows_q = rows // n_q
    me_pair = lax.axis_index("pair")
    q = lax.axis_index("parts") * n_aux + lax.axis_index("aux")
    piece = lax.dynamic_slice_in_dim(v_local, q * rows_q, rows_q, 0)
    carried = jnp.concatenate([piece, sel_flat.reshape(sel_rows, a_width)], 0)
    stage1 = lax.all_gather(carried, "pair", axis=0)

    half = jnp.einsum(
        "kmj,pmn->pkjn", occ_left, cholesky, preferred_element_type=jnp.float32
    ).astype(jnp.bfloat16)
    own = transform(half, v_local[None]).transpose(0, 2, 1, 3)
    stage1, half, own = lax.optimization_barrier((stage1, half, own))
    pair_vectors = jnp.zeros((vectors, occupied, 2, virtuals), jnp.bfloat16)
    pair_vectors = lax.dynamic_update_slice_in_dim(pair_vectors, own, me_pair * a_width, 3)

    sel_pair = stage1[:, rows_q:].reshape(n_pair, -1)[:, :sel_size]
    gathered = gather_group(sel_pair, ("aux",), (n_aux,))
    count = n_aux * n_pair * vectors
    half_rows = gathered.reshape(count * batch, 4, orbitals).transpose(1, 0, 2)
    sel_own = transform(half_rows[None], v_local[None])
    sel_own = sel_own.reshape(2, count, batch, a_width)

    pieces = stage1[:, :rows_q]
    others = (me_pair + jnp.arange(1, n_pair)) % n_pair
    send = jnp.take(pieces, others, axis=0)
    plane = gather_group(send, ("parts", "aux"), (n_parts, n_aux))
    v_others = plane.transpose(1, 0, 2, 3).reshape(n_pair - 1, rows, a_width)
    done = transform(half, v_others).transpose(0, 2, 1, 3)
    for step in range(1, n_pair):
        block = others[step - 1]
        cols = done[..., (step - 1) * a_width:step * a_width]
        pair_vectors = lax.dynamic_update_slice_in_dim(pair_vectors, cols, block * a_width, 3)

    sel_a = sel_own.transpose(1, 2, 0, 3)
    if n_aux == n_pair:
        perm = [(a * n_pair + z, z * n_pair + a) for a in range(n_aux) for z in range(n_pair)]
        sel_b = lax.ppermute(sel_a, ("aux", "pair"), perm)
    else:
        sel_all = lax.all_gather(sel_a, "pair", axis=0)
        sel_b = lax.dynamic_slice_in_dim(sel_all, lax.axis_index("aux") * per_b, per_b, 0)
        sel_b = sel_b.transpose(1, 2, 3, 0, 4).reshape(count, batch, 2, b_width)
    coulomb = pair_terms(sel_b, sel_a)
    paired = coulomb - jnp.swapaxes(coulomb, 2, 3)

    a_start = lax.axis_index("pair") * a_width
    b_start = lax.axis_index("aux") * b_width
    occ_e = jnp.take(occ_energy, batch_occ)
    vir_first = lax.dynamic_slice_in_dim(vir_energy, a_start, a_width)
    vir_second = lax.dynamic_slice_in_dim(vir_energy, b_start, b_width)
    denominator = (
        (occ_e[:, None] + occ_e[None, :])[None, None, :, :, None]
        - vir_first[None, None, None, None, :]
        - vir_second[:, None, None, None, None]
    )
    amplitudes = paired / denominator
    return (pair_vectors, amplitudes)


def solution(mesh):
    return jax.shard_map(
        on_device,
        mesh=mesh,
        in_specs=(
            P(("parts", "aux", "pair"), None, None),
            P(),
            P(None, None, None, "pair"),
            P(),
            P(),
            P(),
        ),
        out_specs=(
            P(("parts", "aux", "pair"), None, None, None),
            P(("parts", "aux"), None, None, None, "pair"),
        ),
        check_vma=False,
    )
```

```python
import functools

import jax
import jax.numpy as jnp
from jax import lax
from jax.experimental import pallas as pl
from jax.experimental.pallas import tpu as pltpu
from jax.sharding import PartitionSpec as P


def transform_kernel(orbitals, h_ref, v_ref, o_ref):
    pn, _, m, n = h_ref.shape
    real = None
    imag = None
    for s in range(2):
        hr = h_ref[:, s].reshape(pn * m, n)
        hi = h_ref[:, 2 + s].reshape(pn * m, n)
        vr = v_ref[0, s * orbitals:(s + 1) * orbitals, :]
        vi = v_ref[0, (2 + s) * orbitals:(3 + s) * orbitals, :]
        rr = jnp.dot(hr, vr, preferred_element_type=jnp.float32)
        ii = jnp.dot(hi, vi, preferred_element_type=jnp.float32)
        ri = jnp.dot(hr, vi, preferred_element_type=jnp.float32)
        ir = jnp.dot(hi, vr, preferred_element_type=jnp.float32)
        real = rr - ii if real is None else real + rr - ii
        imag = ri + ir if imag is None else imag + ri + ir
    w = real.shape[1]
    o_ref[:, 0] = real.reshape(pn, m, w).astype(o_ref.dtype)
    o_ref[:, 1] = imag.reshape(pn, m, w).astype(o_ref.dtype)


def transform(half, v_blocks):
    pn, _, m, n = half.shape
    b, rows, w = v_blocks.shape
    if w % 128 != 0:
        v = v_blocks.reshape(b, 2, 2, n, w)
        hr, hi = half[:, :2], half[:, 2:]
        dims = "pskn,bsnw->pkbw"
        real = jnp.einsum(dims, hr, v[:, 0], preferred_element_type=jnp.float32) - jnp.einsum(
            dims, hi, v[:, 1], preferred_element_type=jnp.float32)
        imag = jnp.einsum(dims, hr, v[:, 1], preferred_element_type=jnp.float32) + jnp.einsum(
            dims, hi, v[:, 0], preferred_element_type=jnp.float32)
        out = jnp.stack([real, imag], 1).astype(jnp.bfloat16)
        return out.reshape(pn, 2, m, b * w)
    flops = 16 * pn * m * n * w * b
    bytes_accessed = 2 * (half.size + v_blocks.size + pn * 2 * m * b * w)
    return pl.pallas_call(
        functools.partial(transform_kernel, n),
        grid=(b,),
        in_specs=[
            pl.BlockSpec((pn, 4, m, n), lambda i: (0, 0, 0, 0)),
            pl.BlockSpec((1, rows, w), lambda i: (i, 0, 0)),
        ],
        out_specs=pl.BlockSpec((pn, 2, m, w), lambda i: (0, 0, 0, i)),
        out_shape=jax.ShapeDtypeStruct((pn, 2, m, b * w), jnp.bfloat16),
        cost_estimate=pl.CostEstimate(flops=flops, bytes_accessed=bytes_accessed, transcendentals=0),
    )(half, v_blocks)


def pair_terms(batch_rows, column_rows):
    left = jnp.concatenate([batch_rows[:, :, 0, :], batch_rows[:, :, 1, :]], 0)
    real_right = jnp.concatenate([column_rows[:, :, 0, :], -column_rows[:, :, 1, :]], 0)
    imag_right = jnp.concatenate([column_rows[:, :, 1, :], column_rows[:, :, 0, :]], 0)
    right = jnp.stack([real_right, imag_right], 1)
    return jnp.einsum("pjb,pcia->bcija", left, right, preferred_element_type=jnp.float32)


def gather_group(x, axes, sizes):
    n = 1
    for size in sizes:
        n *= size
    if n > 16:
        return lax.all_gather(x, axes, axis=0)
    me = lax.axis_index(axes[0])
    for name, size in zip(axes[1:], sizes[1:]):
        me = me * size + lax.axis_index(name)
    blocks = [x]
    for shift in range(1, n):
        perm = [(i, (i + shift) % n) for i in range(n)]
        blocks.append(lax.ppermute(x, axes, perm))
    stacked = jnp.stack(blocks, 0)
    return jnp.take(stacked, (me - jnp.arange(n)) % n, axis=0)


def on_device(cholesky, occ_coef, vir_coef, occ_energy, vir_energy, batch_occ):
    vectors = cholesky.shape[0]
    orbitals = cholesky.shape[1]
    occupied = occ_coef.shape[3]
    a_width = vir_coef.shape[3]
    n_pair = lax.axis_size("pair")
    n_aux = lax.axis_size("aux")
    n_parts = lax.axis_size("parts")
    rows = 4 * orbitals
    virtuals = n_pair * a_width
    b_width = virtuals // n_aux
    per_b = b_width // a_width
    batch = batch_occ.shape[0]

    occ_left = jnp.concatenate([occ_coef[0], -occ_coef[1]], 0)
    v_local = vir_coef.reshape(rows, a_width)

    occ_sel = jnp.take(occ_left, batch_occ, axis=2)
    half_sel = jnp.einsum(
        "kmi,pmn->pikn", occ_sel, cholesky, preferred_element_type=jnp.float32
    ).astype(jnp.bfloat16)
    sel_size = half_sel.size
    sel_rows = -(-sel_size // a_width)
    sel_flat = jnp.pad(half_sel.reshape(-1), (0, sel_rows * a_width - sel_size))

    n_q = n_parts * n_aux
    rows_q = rows // n_q
    me_pair = lax.axis_index("pair")
    q = lax.axis_index("parts") * n_aux + lax.axis_index("aux")
    piece = lax.dynamic_slice_in_dim(v_local, q * rows_q, rows_q, 0)
    carried = jnp.concatenate([piece, sel_flat.reshape(sel_rows, a_width)], 0)
    stage1 = gather_group(carried, ("pair",), (n_pair,))

    half = jnp.einsum(
        "kmj,pmn->pkjn", occ_left, cholesky, preferred_element_type=jnp.float32
    ).astype(jnp.bfloat16)
    own = transform(half, v_local[None]).transpose(0, 2, 1, 3)
    stage1, half, own = lax.optimization_barrier((stage1, half, own))
    pair_vectors = jnp.zeros((vectors, occupied, 2, virtuals), jnp.bfloat16)
    pair_vectors = lax.dynamic_update_slice_in_dim(pair_vectors, own, me_pair * a_width, 3)

    sel_pair = stage1[:, rows_q:].reshape(n_pair, -1)[:, :sel_size]
    gathered = gather_group(sel_pair, ("aux",), (n_aux,))
    count = n_aux * n_pair * vectors
    half_rows = gathered.reshape(count * batch, 4, orbitals).transpose(1, 0, 2)
    sel_own = transform(half_rows[None], v_local[None])
    sel_own = sel_own.reshape(2, count, batch, a_width)

    pieces = stage1[:, :rows_q]
    others = (me_pair + jnp.arange(1, n_pair)) % n_pair
    send = jnp.take(pieces, others, axis=0)
    plane = lax.all_gather(send, ("parts", "aux"), axis=0)
    v_others = plane.transpose(1, 0, 2, 3).reshape(n_pair - 1, rows, a_width)
    done = transform(half, v_others).transpose(0, 2, 1, 3)
    for step in range(1, n_pair):
        block = others[step - 1]
        cols = done[..., (step - 1) * a_width:step * a_width]
        pair_vectors = lax.dynamic_update_slice_in_dim(pair_vectors, cols, block * a_width, 3)

    sel_a = sel_own.transpose(1, 2, 0, 3)
    if n_aux == n_pair:
        perm = [(a * n_pair + z, z * n_pair + a) for a in range(n_aux) for z in range(n_pair)]
        sel_b = lax.ppermute(sel_a, ("aux", "pair"), perm)
    else:
        sel_all = lax.all_gather(sel_a, "pair", axis=0)
        sel_b = lax.dynamic_slice_in_dim(sel_all, lax.axis_index("aux") * per_b, per_b, 0)
        sel_b = sel_b.transpose(1, 2, 3, 0, 4).reshape(count, batch, 2, b_width)
    coulomb = pair_terms(sel_b, sel_a)
    paired = coulomb - jnp.swapaxes(coulomb, 2, 3)

    a_start = lax.axis_index("pair") * a_width
    b_start = lax.axis_index("aux") * b_width
    occ_e = jnp.take(occ_energy, batch_occ)
    vir_first = lax.dynamic_slice_in_dim(vir_energy, a_start, a_width)
    vir_second = lax.dynamic_slice_in_dim(vir_energy, b_start, b_width)
    denominator = (
        (occ_e[:, None] + occ_e[None, :])[None, None, :, :, None]
        - vir_first[None, None, None, None, :]
        - vir_second[:, None, None, None, None]
    )
    amplitudes = paired / denominator
    return (pair_vectors, amplitudes)


def solution(mesh):
    return jax.shard_map(
        on_device,
        mesh=mesh,
        in_specs=(
            P(("parts", "aux", "pair"), None, None),
            P(),
            P(None, None, None, "pair"),
            P(),
            P(),
            P(),
        ),
        out_specs=(
            P(("parts", "aux", "pair"), None, None, None),
            P(("parts", "aux"), None, None, None, "pair"),
        ),
        check_vma=False,
    )
```

```python
import functools

import jax
import jax.numpy as jnp
from jax import lax
from jax.experimental import pallas as pl
from jax.experimental.pallas import tpu as pltpu
from jax.sharding import PartitionSpec as P


def transform_kernel(orbitals, h_ref, v_ref, o_ref):
    pn, _, m, n = h_ref.shape
    real = None
    imag = None
    for s in range(2):
        hr = h_ref[:, s].reshape(pn * m, n)
        hi = h_ref[:, 2 + s].reshape(pn * m, n)
        vr = v_ref[0, s * orbitals:(s + 1) * orbitals, :]
        vi = v_ref[0, (2 + s) * orbitals:(3 + s) * orbitals, :]
        rr = jnp.dot(hr, vr, preferred_element_type=jnp.float32)
        ii = jnp.dot(hi, vi, preferred_element_type=jnp.float32)
        ri = jnp.dot(hr, vi, preferred_element_type=jnp.float32)
        ir = jnp.dot(hi, vr, preferred_element_type=jnp.float32)
        real = rr - ii if real is None else real + rr - ii
        imag = ri + ir if imag is None else imag + ri + ir
    w = real.shape[1]
    o_ref[:, 0] = real.reshape(pn, m, w).astype(o_ref.dtype)
    o_ref[:, 1] = imag.reshape(pn, m, w).astype(o_ref.dtype)


def transform(half, v_blocks):
    pn, _, m, n = half.shape
    b, rows, w = v_blocks.shape
    if w % 128 != 0:
        v = v_blocks.reshape(b, 2, 2, n, w)
        hr, hi = half[:, :2], half[:, 2:]
        dims = "pskn,bsnw->pkbw"
        real = jnp.einsum(dims, hr, v[:, 0], preferred_element_type=jnp.float32) - jnp.einsum(
            dims, hi, v[:, 1], preferred_element_type=jnp.float32)
        imag = jnp.einsum(dims, hr, v[:, 1], preferred_element_type=jnp.float32) + jnp.einsum(
            dims, hi, v[:, 0], preferred_element_type=jnp.float32)
        out = jnp.stack([real, imag], 1).astype(jnp.bfloat16)
        return out.reshape(pn, 2, m, b * w)
    flops = 16 * pn * m * n * w * b
    bytes_accessed = 2 * (half.size + v_blocks.size + pn * 2 * m * b * w)
    return pl.pallas_call(
        functools.partial(transform_kernel, n),
        grid=(b,),
        in_specs=[
            pl.BlockSpec((pn, 4, m, n), lambda i: (0, 0, 0, 0)),
            pl.BlockSpec((1, rows, w), lambda i: (i, 0, 0)),
        ],
        out_specs=pl.BlockSpec((pn, 2, m, w), lambda i: (0, 0, 0, i)),
        out_shape=jax.ShapeDtypeStruct((pn, 2, m, b * w), jnp.bfloat16),
        cost_estimate=pl.CostEstimate(flops=flops, bytes_accessed=bytes_accessed, transcendentals=0),
    )(half, v_blocks)


def pair_terms(batch_rows, column_rows):
    left = jnp.concatenate([batch_rows[:, :, 0, :], batch_rows[:, :, 1, :]], 0)
    real_right = jnp.concatenate([column_rows[:, :, 0, :], -column_rows[:, :, 1, :]], 0)
    imag_right = jnp.concatenate([column_rows[:, :, 1, :], column_rows[:, :, 0, :]], 0)
    right = jnp.stack([real_right, imag_right], 1)
    return jnp.einsum("pjb,pcia->bcija", left, right, preferred_element_type=jnp.float32)


def gather_group(x, axes, sizes):
    n = 1
    for size in sizes:
        n *= size
    if n > 16:
        return lax.all_gather(x, axes, axis=0)
    me = lax.axis_index(axes[0])
    for name, size in zip(axes[1:], sizes[1:]):
        me = me * size + lax.axis_index(name)
    blocks = [x]
    for shift in range(1, n):
        perm = [(i, (i + shift) % n) for i in range(n)]
        blocks.append(lax.ppermute(x, axes, perm))
    stacked = jnp.stack(blocks, 0)
    return jnp.take(stacked, (me - jnp.arange(n)) % n, axis=0)


def on_device(cholesky, occ_coef, vir_coef, occ_energy, vir_energy, batch_occ):
    vectors = cholesky.shape[0]
    orbitals = cholesky.shape[1]
    occupied = occ_coef.shape[3]
    a_width = vir_coef.shape[3]
    n_pair = lax.axis_size("pair")
    n_aux = lax.axis_size("aux")
    n_parts = lax.axis_size("parts")
    rows = 4 * orbitals
    virtuals = n_pair * a_width
    b_width = virtuals // n_aux
    per_b = b_width // a_width
    batch = batch_occ.shape[0]

    occ_left = jnp.concatenate([occ_coef[0], -occ_coef[1]], 0)
    v_local = vir_coef.reshape(rows, a_width)

    occ_sel = jnp.take(occ_left, batch_occ, axis=2)
    half_sel = jnp.einsum(
        "kmi,pmn->pikn", occ_sel, cholesky, preferred_element_type=jnp.float32
    ).astype(jnp.bfloat16)
    by_pair = gather_group(half_sel, ("pair",), (n_pair,))
    gathered = gather_group(by_pair, ("aux",), (n_aux,))
    count = n_aux * n_pair * vectors
    half_rows = gathered.reshape(count * batch, 4, orbitals).transpose(1, 0, 2)
    sel_own = transform(half_rows[None], v_local[None])
    sel_own = sel_own.reshape(2, count, batch, a_width)

    n_q = n_parts * n_aux
    rows_q = rows // n_q
    q = lax.axis_index("parts") * n_aux + lax.axis_index("aux")
    piece = lax.dynamic_slice_in_dim(v_local, q * rows_q, rows_q, 0)
    v_full = lax.all_gather(piece, ("pair", "parts", "aux"), axis=0, tiled=True)
    v_full = v_full.reshape(n_pair, rows, a_width)
    half = jnp.einsum(
        "kmj,pmn->pkjn", occ_left, cholesky, preferred_element_type=jnp.float32
    ).astype(jnp.bfloat16)
    pair_vectors = transform(half, v_full).transpose(0, 2, 1, 3)

    sel_a = sel_own.transpose(1, 2, 0, 3)
    if n_aux == n_pair:
        perm = [(a * n_pair + z, z * n_pair + a) for a in range(n_aux) for z in range(n_pair)]
        sel_b = lax.ppermute(sel_a, ("aux", "pair"), perm)
    else:
        sel_all = lax.all_gather(sel_a, "pair", axis=0)
        sel_b = lax.dynamic_slice_in_dim(sel_all, lax.axis_index("aux") * per_b, per_b, 0)
        sel_b = sel_b.transpose(1, 2, 3, 0, 4).reshape(count, batch, 2, b_width)
    coulomb = pair_terms(sel_b, sel_a)
    paired = coulomb - jnp.swapaxes(coulomb, 2, 3)

    a_start = lax.axis_index("pair") * a_width
    b_start = lax.axis_index("aux") * b_width
    occ_e = jnp.take(occ_energy, batch_occ)
    vir_first = lax.dynamic_slice_in_dim(vir_energy, a_start, a_width)
    vir_second = lax.dynamic_slice_in_dim(vir_energy, b_start, b_width)
    denominator = (
        (occ_e[:, None] + occ_e[None, :])[None, None, :, :, None]
        - vir_first[None, None, None, None, :]
        - vir_second[:, None, None, None, None]
    )
    amplitudes = paired / denominator
    return (pair_vectors, amplitudes)


def solution(mesh):
    return jax.shard_map(
        on_device,
        mesh=mesh,
        in_specs=(
            P(("parts", "aux", "pair"), None, None),
            P(),
            P(None, None, None, "pair"),
            P(),
            P(),
            P(),
        ),
        out_specs=(
            P(("parts", "aux", "pair"), None, None, None),
            P(("parts", "aux"), None, None, None, "pair"),
        ),
        check_vma=False,
    )
```

```python
import functools

import jax
import jax.numpy as jnp
from jax import lax
from jax.experimental import pallas as pl
from jax.experimental.pallas import tpu as pltpu
from jax.sharding import PartitionSpec as P


def transform_kernel(orbitals, flag_ref, h_ref, a_ref, b_ref, o_ref):
    pn, _, m, n = h_ref.shape
    terms = [None] * 4
    for s in range(2):
        hr = h_ref[:, s].reshape(pn * m, n)
        hi = h_ref[:, 2 + s].reshape(pn * m, n)
        va = a_ref[0, s * orbitals:(s + 1) * orbitals, :]
        vb = b_ref[0, s * orbitals:(s + 1) * orbitals, :]
        parts = (hr, va), (hi, vb), (hr, vb), (hi, va)
        for t, (x, y) in enumerate(parts):
            d = jnp.dot(x, y, preferred_element_type=jnp.float32)
            terms[t] = d if terms[t] is None else terms[t] + d
    straight = flag_ref[0] == 0
    real = jnp.where(straight, terms[0] - terms[1], terms[2] - terms[3])
    imag = jnp.where(straight, terms[2] + terms[3], terms[0] + terms[1])
    w = real.shape[1]
    o_ref[:, 0] = real.reshape(pn, m, w).astype(o_ref.dtype)
    o_ref[:, 1] = imag.reshape(pn, m, w).astype(o_ref.dtype)


def transform(half, a_blocks, b_blocks, flag):
    pn, _, m, n = half.shape
    b, rows, w = a_blocks.shape
    flag = jnp.asarray(flag, jnp.int32).reshape(1)
    if w % 128 != 0:
        va = a_blocks.reshape(b, 2, n, w)
        vb = b_blocks.reshape(b, 2, n, w)
        hr, hi = half[:, :2], half[:, 2:]
        dims = "pskn,bsnw->pkbw"
        t0 = jnp.einsum(dims, hr, va, preferred_element_type=jnp.float32)
        t1 = jnp.einsum(dims, hi, vb, preferred_element_type=jnp.float32)
        t2 = jnp.einsum(dims, hr, vb, preferred_element_type=jnp.float32)
        t3 = jnp.einsum(dims, hi, va, preferred_element_type=jnp.float32)
        straight = flag[0] == 0
        real = jnp.where(straight, t0 - t1, t2 - t3)
        imag = jnp.where(straight, t2 + t3, t0 + t1)
        out = jnp.stack([real, imag], 1).astype(jnp.bfloat16)
        return out.reshape(pn, 2, m, b * w)
    flops = 16 * pn * m * n * w * b
    bytes_accessed = 2 * (half.size + 2 * a_blocks.size + pn * 2 * m * b * w)
    return pl.pallas_call(
        functools.partial(transform_kernel, n),
        grid=(b,),
        in_specs=[
            pl.BlockSpec(memory_space=pltpu.SMEM),
            pl.BlockSpec((pn, 4, m, n), lambda i: (0, 0, 0, 0)),
            pl.BlockSpec((1, rows, w), lambda i: (i, 0, 0)),
            pl.BlockSpec((1, rows, w), lambda i: (i, 0, 0)),
        ],
        out_specs=pl.BlockSpec((pn, 2, m, w), lambda i: (0, 0, 0, i)),
        out_shape=jax.ShapeDtypeStruct((pn, 2, m, b * w), jnp.bfloat16),
        cost_estimate=pl.CostEstimate(flops=flops, bytes_accessed=bytes_accessed, transcendentals=0),
    )(flag, half, a_blocks, b_blocks)


def pair_terms(batch_rows, column_rows):
    left = jnp.concatenate([batch_rows[:, :, 0, :], batch_rows[:, :, 1, :]], 0)
    real_right = jnp.concatenate([column_rows[:, :, 0, :], -column_rows[:, :, 1, :]], 0)
    imag_right = jnp.concatenate([column_rows[:, :, 1, :], column_rows[:, :, 0, :]], 0)
    right = jnp.stack([real_right, imag_right], 1)
    return jnp.einsum("pjb,pcia->bcija", left, right, preferred_element_type=jnp.float32)


def gather_group(x, axes, sizes):
    n = 1
    for size in sizes:
        n *= size
    if n > 16:
        return lax.all_gather(x, axes, axis=0)
    me = lax.axis_index(axes[0])
    for name, size in zip(axes[1:], sizes[1:]):
        me = me * size + lax.axis_index(name)
    blocks = [x]
    for shift in range(1, n):
        perm = [(i, (i + shift) % n) for i in range(n)]
        blocks.append(lax.ppermute(x, axes, perm))
    stacked = jnp.stack(blocks, 0)
    return jnp.take(stacked, (me - jnp.arange(n)) % n, axis=0)


AUX = ("x", "core")


def on_device(cholesky, occ_coef, vir_coef, occ_energy, vir_energy, batch_occ):
    vectors = cholesky.shape[0]
    orbitals = cholesky.shape[1]
    occupied = occ_coef.shape[3]
    a_width = vir_coef.shape[3]
    n_pair = lax.axis_size("pair")
    n_core = lax.axis_size("core")
    n_aux = lax.axis_size("x") * n_core
    aux_index = lax.axis_index("x") * n_core + lax.axis_index("core")
    n_parts = lax.axis_size("parts")
    rows = 4 * orbitals
    virtuals = n_pair * a_width
    b_width = virtuals // n_aux
    per_b = b_width // a_width
    batch = batch_occ.shape[0]

    occ_left = jnp.concatenate([occ_coef[0], -occ_coef[1]], 0)
    v_local = vir_coef.reshape(rows, a_width)

    occ_sel = jnp.take(occ_left, batch_occ, axis=2)
    half_sel = jnp.einsum(
        "kmi,pmn->pikn", occ_sel, cholesky, preferred_element_type=jnp.float32
    ).astype(jnp.bfloat16)
    by_pair = gather_group(half_sel, ("pair",), (n_pair,))
    gathered = gather_group(by_pair, AUX, (n_aux // n_core, n_core))
    count = n_aux * n_pair * vectors
    half_rows = gathered.reshape(count * batch, 4, orbitals).transpose(1, 0, 2)
    v_halves = v_local.reshape(2, 1, rows // 2, a_width)
    sel_own = transform(half_rows[None], v_halves[0], v_halves[1], 0)
    sel_own = sel_own.reshape(2, count, batch, a_width)

    n_q = n_parts * n_aux
    rows_q = rows // n_q
    n_x = n_aux // n_core
    me_core = lax.axis_index("core")
    q = me_core * (n_parts * n_x) + lax.axis_index("parts") * n_x + lax.axis_index("x")
    piece = lax.dynamic_slice_in_dim(v_local, q * rows_q, rows_q, 0)
    mine = lax.all_gather(piece, ("pair", "parts", "x"), axis=0)
    mine = mine.reshape(n_pair, rows // n_core, a_width)
    other = lax.ppermute(mine, "core", [(c, (c + 1) % n_core) for c in range(n_core)])
    half = jnp.einsum(
        "kmj,pmn->pkjn", occ_left, cholesky, preferred_element_type=jnp.float32
    ).astype(jnp.bfloat16)
    pair_vectors = transform(half, mine, other, me_core).transpose(0, 2, 1, 3)

    sel_a = sel_own.transpose(1, 2, 0, 3)
    if n_aux == n_pair:
        perm = [(a * n_pair + z, z * n_pair + a) for a in range(n_aux) for z in range(n_pair)]
        sel_b = lax.ppermute(sel_a, AUX + ("pair",), perm)
    else:
        sel_all = lax.all_gather(sel_a, "pair", axis=0)
        sel_b = lax.dynamic_slice_in_dim(sel_all, aux_index * per_b, per_b, 0)
        sel_b = sel_b.transpose(1, 2, 3, 0, 4).reshape(count, batch, 2, b_width)
    coulomb = pair_terms(sel_b, sel_a)
    paired = coulomb - jnp.swapaxes(coulomb, 2, 3)

    a_start = lax.axis_index("pair") * a_width
    b_start = aux_index * b_width
    occ_e = jnp.take(occ_energy, batch_occ)
    vir_first = lax.dynamic_slice_in_dim(vir_energy, a_start, a_width)
    vir_second = lax.dynamic_slice_in_dim(vir_energy, b_start, b_width)
    denominator = (
        (occ_e[:, None] + occ_e[None, :])[None, None, :, :, None]
        - vir_first[None, None, None, None, :]
        - vir_second[:, None, None, None, None]
    )
    amplitudes = paired / denominator
    return (pair_vectors, amplitudes)


def solution(mesh):
    sizes = dict(zip(mesh.axis_names, mesh.devices.shape))
    cores = 2
    devices = mesh.devices.reshape(sizes["parts"], sizes["aux"] // cores, cores, sizes["pair"])
    split = jax.sharding.Mesh(devices, ("parts", "x", "core", "pair"))
    return jax.shard_map(
        on_device,
        mesh=split,
        in_specs=(
            P(("parts",) + AUX + ("pair",), None, None),
            P(),
            P(None, None, None, "pair"),
            P(),
            P(),
            P(),
        ),
        out_specs=(
            P(("parts",) + AUX + ("pair",), None, None, None),
            P(("parts",) + AUX, None, None, None, "pair"),
        ),
        check_vma=False,
    )
```

```python
import functools

import jax
import jax.numpy as jnp
from jax import lax
from jax.experimental import pallas as pl
from jax.experimental.pallas import tpu as pltpu
from jax.sharding import PartitionSpec as P


def transform_kernel(h_ref, v_ref, o_ref):
    pn, _, m, k = h_ref.shape
    hr = h_ref[:, 0].reshape(pn * m, k)
    hi = h_ref[:, 1].reshape(pn * m, k)
    vr = v_ref[0, :k, :]
    vi = v_ref[0, k:, :]
    real = jnp.dot(hr, vr, preferred_element_type=jnp.float32) - jnp.dot(
        hi, vi, preferred_element_type=jnp.float32)
    imag = jnp.dot(hr, vi, preferred_element_type=jnp.float32) + jnp.dot(
        hi, vr, preferred_element_type=jnp.float32)
    w = real.shape[1]
    o_ref[:, 0] = real.reshape(pn, m, w).astype(o_ref.dtype)
    o_ref[:, 1] = imag.reshape(pn, m, w).astype(o_ref.dtype)


def merge_spin(half):
    pn, _, m, n = half.shape
    return half.reshape(pn, 2, 2, m, n).transpose(0, 1, 3, 2, 4).reshape(pn, 2, m, 2 * n)


def transform(half, v_blocks):
    pn, _, m, k = half.shape
    b, rows, w = v_blocks.shape
    if w % 128 != 0:
        v = v_blocks.reshape(b, 2, k, w)
        hr, hi = half[:, 0], half[:, 1]
        dims = "pmk,bkw->pmbw"
        real = jnp.einsum(dims, hr, v[:, 0], preferred_element_type=jnp.float32) - jnp.einsum(
            dims, hi, v[:, 1], preferred_element_type=jnp.float32)
        imag = jnp.einsum(dims, hr, v[:, 1], preferred_element_type=jnp.float32) + jnp.einsum(
            dims, hi, v[:, 0], preferred_element_type=jnp.float32)
        out = jnp.stack([real, imag], 1).astype(jnp.bfloat16)
        return out.reshape(pn, 2, m, b * w)
    flops = 8 * pn * m * k * w * b
    bytes_accessed = 2 * (half.size + v_blocks.size + pn * 2 * m * b * w)
    return pl.pallas_call(
        transform_kernel,
        grid=(b,),
        in_specs=[
            pl.BlockSpec((pn, 2, m, k), lambda i: (0, 0, 0, 0)),
            pl.BlockSpec((1, rows, w), lambda i: (i, 0, 0)),
        ],
        out_specs=pl.BlockSpec((pn, 2, m, w), lambda i: (0, 0, 0, i)),
        out_shape=jax.ShapeDtypeStruct((pn, 2, m, b * w), jnp.bfloat16),
        cost_estimate=pl.CostEstimate(flops=flops, bytes_accessed=bytes_accessed, transcendentals=0),
    )(half, v_blocks)


def pair_terms(batch_rows, column_rows):
    left = jnp.concatenate([batch_rows[:, :, 0, :], batch_rows[:, :, 1, :]], 0)
    real_right = jnp.concatenate([column_rows[:, :, 0, :], -column_rows[:, :, 1, :]], 0)
    imag_right = jnp.concatenate([column_rows[:, :, 1, :], column_rows[:, :, 0, :]], 0)
    right = jnp.stack([real_right, imag_right], 1)
    return jnp.einsum("pjb,pcia->bcija", left, right, preferred_element_type=jnp.float32)


def gather_group(x, axes, sizes):
    n = 1
    for size in sizes:
        n *= size
    if n > 16:
        return lax.all_gather(x, axes, axis=0)
    me = lax.axis_index(axes[0])
    for name, size in zip(axes[1:], sizes[1:]):
        me = me * size + lax.axis_index(name)
    blocks = [x]
    for shift in range(1, n):
        perm = [(i, (i + shift) % n) for i in range(n)]
        blocks.append(lax.ppermute(x, axes, perm))
    stacked = jnp.stack(blocks, 0)
    return jnp.take(stacked, (me - jnp.arange(n)) % n, axis=0)


def on_device(cholesky, occ_coef, vir_coef, occ_energy, vir_energy, batch_occ):
    vectors = cholesky.shape[0]
    orbitals = cholesky.shape[1]
    occupied = occ_coef.shape[3]
    a_width = vir_coef.shape[3]
    n_pair = lax.axis_size("pair")
    n_aux = lax.axis_size("aux")
    n_parts = lax.axis_size("parts")
    rows = 4 * orbitals
    virtuals = n_pair * a_width
    b_width = virtuals // n_aux
    per_b = b_width // a_width
    batch = batch_occ.shape[0]

    occ_left = jnp.concatenate([occ_coef[0], -occ_coef[1]], 0)
    v_local = vir_coef.reshape(rows, a_width)

    occ_sel = jnp.take(occ_left, batch_occ, axis=2)
    half_sel = jnp.einsum(
        "kmi,pmn->pikn", occ_sel, cholesky, preferred_element_type=jnp.float32
    ).astype(jnp.bfloat16)
    by_pair = gather_group(half_sel, ("pair",), (n_pair,))
    gathered = gather_group(by_pair, ("aux",), (n_aux,))
    count = n_aux * n_pair * vectors
    half_rows = gathered.reshape(count * batch, 4, orbitals).transpose(1, 0, 2)
    sel_own = transform(merge_spin(half_rows[None]), v_local[None])
    sel_own = sel_own.reshape(2, count, batch, a_width)

    n_q = n_parts * n_aux
    rows_q = rows // n_q
    q = lax.axis_index("parts") * n_aux + lax.axis_index("aux")
    piece = lax.dynamic_slice_in_dim(v_local, q * rows_q, rows_q, 0)
    v_full = lax.all_gather(piece, ("pair", "parts", "aux"), axis=0, tiled=True)
    v_full = v_full.reshape(n_pair, rows, a_width)
    half = jnp.einsum(
        "kmj,pmn->pkjn", occ_left, cholesky, preferred_element_type=jnp.float32
    ).astype(jnp.bfloat16)
    pair_vectors = transform(merge_spin(half), v_full).transpose(0, 2, 1, 3)

    sel_a = sel_own.transpose(1, 2, 0, 3)
    if n_aux == n_pair:
        perm = [(a * n_pair + z, z * n_pair + a) for a in range(n_aux) for z in range(n_pair)]
        sel_b = lax.ppermute(sel_a, ("aux", "pair"), perm)
    else:
        sel_all = lax.all_gather(sel_a, "pair", axis=0)
        sel_b = lax.dynamic_slice_in_dim(sel_all, lax.axis_index("aux") * per_b, per_b, 0)
        sel_b = sel_b.transpose(1, 2, 3, 0, 4).reshape(count, batch, 2, b_width)
    coulomb = pair_terms(sel_b, sel_a)
    paired = coulomb - jnp.swapaxes(coulomb, 2, 3)

    a_start = lax.axis_index("pair") * a_width
    b_start = lax.axis_index("aux") * b_width
    occ_e = jnp.take(occ_energy, batch_occ)
    vir_first = lax.dynamic_slice_in_dim(vir_energy, a_start, a_width)
    vir_second = lax.dynamic_slice_in_dim(vir_energy, b_start, b_width)
    denominator = (
        (occ_e[:, None] + occ_e[None, :])[None, None, :, :, None]
        - vir_first[None, None, None, None, :]
        - vir_second[:, None, None, None, None]
    )
    amplitudes = paired / denominator
    return (pair_vectors, amplitudes)


def solution(mesh):
    return jax.shard_map(
        on_device,
        mesh=mesh,
        in_specs=(
            P(("parts", "aux", "pair"), None, None),
            P(),
            P(None, None, None, "pair"),
            P(),
            P(),
            P(),
        ),
        out_specs=(
            P(("parts", "aux", "pair"), None, None, None),
            P(("parts", "aux"), None, None, None, "pair"),
        ),
        check_vma=False,
    )
```

```python
import functools

import jax
import jax.numpy as jnp
from jax import lax
from jax.experimental import pallas as pl
from jax.experimental.pallas import tpu as pltpu
from jax.sharding import PartitionSpec as P


def transform_kernel(h_ref, v_ref, o_ref):
    pn, _, m, k = h_ref.shape
    hr = h_ref[:, 0].reshape(pn * m, k)
    hi = h_ref[:, 1].reshape(pn * m, k)
    vr = v_ref[0, :k, :]
    vi = v_ref[0, k:, :]
    real = jnp.dot(hr, vr, preferred_element_type=jnp.float32) - jnp.dot(
        hi, vi, preferred_element_type=jnp.float32)
    imag = jnp.dot(hr, vi, preferred_element_type=jnp.float32) + jnp.dot(
        hi, vr, preferred_element_type=jnp.float32)
    w = real.shape[1]
    o_ref[:, 0] = real.reshape(pn, m, w).astype(o_ref.dtype)
    o_ref[:, 1] = imag.reshape(pn, m, w).astype(o_ref.dtype)


def merge_spin(half):
    pn, _, m, n = half.shape
    return half.reshape(pn, 2, 2, m, n).transpose(0, 1, 3, 2, 4).reshape(pn, 2, m, 2 * n)


def transform(half, v_blocks):
    pn, _, m, k = half.shape
    b, rows, w = v_blocks.shape
    if w % 128 != 0:
        v = v_blocks.reshape(b, 2, k, w)
        hr, hi = half[:, 0], half[:, 1]
        dims = "pmk,bkw->pmbw"
        real = jnp.einsum(dims, hr, v[:, 0], preferred_element_type=jnp.float32) - jnp.einsum(
            dims, hi, v[:, 1], preferred_element_type=jnp.float32)
        imag = jnp.einsum(dims, hr, v[:, 1], preferred_element_type=jnp.float32) + jnp.einsum(
            dims, hi, v[:, 0], preferred_element_type=jnp.float32)
        out = jnp.stack([real, imag], 1).astype(jnp.bfloat16)
        return out.reshape(pn, 2, m, b * w)
    flops = 8 * pn * m * k * w * b
    bytes_accessed = 2 * (half.size + v_blocks.size + pn * 2 * m * b * w)
    return pl.pallas_call(
        transform_kernel,
        grid=(b,),
        in_specs=[
            pl.BlockSpec((pn, 2, m, k), lambda i: (0, 0, 0, 0)),
            pl.BlockSpec((1, rows, w), lambda i: (i, 0, 0)),
        ],
        out_specs=pl.BlockSpec((pn, 2, m, w), lambda i: (0, 0, 0, i)),
        out_shape=jax.ShapeDtypeStruct((pn, 2, m, b * w), jnp.bfloat16),
        cost_estimate=pl.CostEstimate(flops=flops, bytes_accessed=bytes_accessed, transcendentals=0),
    )(half, v_blocks)


def transform_from(half, v_blocks, start, count):
    pn, _, m, k = half.shape
    b, rows, w = v_blocks.shape
    if w % 128 != 0:
        picked = jnp.take(v_blocks, (start + jnp.arange(count)) % b, axis=0)
        return transform(half, picked)
    flops = 8 * pn * m * k * w * count
    bytes_accessed = 2 * (half.size + rows * w * count + pn * 2 * m * count * w)
    grid_spec = pltpu.PrefetchScalarGridSpec(
        num_scalar_prefetch=1,
        grid=(count,),
        in_specs=[
            pl.BlockSpec((pn, 2, m, k), lambda i, first: (0, 0, 0, 0)),
            pl.BlockSpec((1, rows, w), lambda i, first: ((first[0] + i) % b, 0, 0)),
        ],
        out_specs=pl.BlockSpec((pn, 2, m, w), lambda i, first: (0, 0, 0, i)),
    )
    return pl.pallas_call(
        lambda first_ref, h_ref, v_ref, o_ref: transform_kernel(h_ref, v_ref, o_ref),
        grid_spec=grid_spec,
        out_shape=jax.ShapeDtypeStruct((pn, 2, m, count * w), jnp.bfloat16),
        cost_estimate=pl.CostEstimate(flops=flops, bytes_accessed=bytes_accessed, transcendentals=0),
    )(jnp.asarray(start, jnp.int32).reshape(1), half, v_blocks)


def pair_terms(batch_rows, column_rows):
    left = jnp.concatenate([batch_rows[:, :, 0, :], batch_rows[:, :, 1, :]], 0)
    real_right = jnp.concatenate([column_rows[:, :, 0, :], -column_rows[:, :, 1, :]], 0)
    imag_right = jnp.concatenate([column_rows[:, :, 1, :], column_rows[:, :, 0, :]], 0)
    right = jnp.stack([real_right, imag_right], 1)
    return jnp.einsum("pjb,pcia->bcija", left, right, preferred_element_type=jnp.float32)


def gather_group(x, axes, sizes):
    n = 1
    for size in sizes:
        n *= size
    if n > 16:
        return lax.all_gather(x, axes, axis=0)
    me = lax.axis_index(axes[0])
    for name, size in zip(axes[1:], sizes[1:]):
        me = me * size + lax.axis_index(name)
    blocks = [x]
    for shift in range(1, n):
        perm = [(i, (i + shift) % n) for i in range(n)]
        blocks.append(lax.ppermute(x, axes, perm))
    stacked = jnp.stack(blocks, 0)
    return jnp.take(stacked, (me - jnp.arange(n)) % n, axis=0)


def on_device(cholesky, occ_coef, vir_coef, occ_energy, vir_energy, batch_occ):
    vectors = cholesky.shape[0]
    orbitals = cholesky.shape[1]
    occupied = occ_coef.shape[3]
    a_width = vir_coef.shape[3]
    n_pair = lax.axis_size("pair")
    n_aux = lax.axis_size("aux")
    n_parts = lax.axis_size("parts")
    rows = 4 * orbitals
    virtuals = n_pair * a_width
    b_width = virtuals // n_aux
    per_b = b_width // a_width
    batch = batch_occ.shape[0]

    occ_left = jnp.concatenate([occ_coef[0], -occ_coef[1]], 0)
    v_local = vir_coef.reshape(rows, a_width)

    occ_sel = jnp.take(occ_left, batch_occ, axis=2)
    half_sel = jnp.einsum(
        "kmi,pmn->pikn", occ_sel, cholesky, preferred_element_type=jnp.float32
    ).astype(jnp.bfloat16)
    by_pair = gather_group(half_sel, ("pair",), (n_pair,))
    gathered = gather_group(by_pair, ("aux",), (n_aux,))
    count = n_aux * n_pair * vectors
    half_rows = gathered.reshape(count * batch, 4, orbitals).transpose(1, 0, 2)
    sel_own = transform(merge_spin(half_rows[None]), v_local[None])
    sel_own = sel_own.reshape(2, count, batch, a_width)

    n_q = n_parts * n_aux
    rows_q = rows // n_q
    q = lax.axis_index("parts") * n_aux + lax.axis_index("aux")
    piece = lax.dynamic_slice_in_dim(v_local, q * rows_q, rows_q, 0)
    v_full = lax.all_gather(piece, ("pair", "parts", "aux"), axis=0, tiled=True)
    v_full = v_full.reshape(n_pair, rows, a_width)
    half = jnp.einsum(
        "kmj,pmn->pkjn", occ_left, cholesky, preferred_element_type=jnp.float32
    ).astype(jnp.bfloat16)
    half_m = merge_spin(half)
    me_pair = lax.axis_index("pair")
    own = transform(half_m, v_local[None]).transpose(0, 2, 1, 3)
    pair_vectors = jnp.zeros((vectors, occupied, 2, n_pair * a_width), jnp.bfloat16)
    pair_vectors = lax.dynamic_update_slice_in_dim(pair_vectors, own, me_pair * a_width, 3)
    rest = transform_from(half_m, v_full, me_pair + 1, n_pair - 1).transpose(0, 2, 1, 3)
    for step in range(1, n_pair):
        block = (me_pair + step) % n_pair
        cols = rest[..., (step - 1) * a_width:step * a_width]
        pair_vectors = lax.dynamic_update_slice_in_dim(pair_vectors, cols, block * a_width, 3)

    sel_a = sel_own.transpose(1, 2, 0, 3)
    if n_aux == n_pair:
        perm = [(a * n_pair + z, z * n_pair + a) for a in range(n_aux) for z in range(n_pair)]
        sel_b = lax.ppermute(sel_a, ("aux", "pair"), perm)
    else:
        sel_all = lax.all_gather(sel_a, "pair", axis=0)
        sel_b = lax.dynamic_slice_in_dim(sel_all, lax.axis_index("aux") * per_b, per_b, 0)
        sel_b = sel_b.transpose(1, 2, 3, 0, 4).reshape(count, batch, 2, b_width)
    coulomb = pair_terms(sel_b, sel_a)
    paired = coulomb - jnp.swapaxes(coulomb, 2, 3)

    a_start = lax.axis_index("pair") * a_width
    b_start = lax.axis_index("aux") * b_width
    occ_e = jnp.take(occ_energy, batch_occ)
    vir_first = lax.dynamic_slice_in_dim(vir_energy, a_start, a_width)
    vir_second = lax.dynamic_slice_in_dim(vir_energy, b_start, b_width)
    denominator = (
        (occ_e[:, None] + occ_e[None, :])[None, None, :, :, None]
        - vir_first[None, None, None, None, :]
        - vir_second[:, None, None, None, None]
    )
    amplitudes = paired / denominator
    return (pair_vectors, amplitudes)


def solution(mesh):
    return jax.shard_map(
        on_device,
        mesh=mesh,
        in_specs=(
            P(("parts", "aux", "pair"), None, None),
            P(),
            P(None, None, None, "pair"),
            P(),
            P(),
            P(),
        ),
        out_specs=(
            P(("parts", "aux", "pair"), None, None, None),
            P(("parts", "aux"), None, None, None, "pair"),
        ),
        check_vma=False,
    )
```

```python
import functools

import jax
import jax.numpy as jnp
from jax import lax
from jax.experimental import pallas as pl
from jax.experimental.pallas import tpu as pltpu
from jax.sharding import PartitionSpec as P


def transform_kernel(split, h_ref, top_ref, bot_ref, o_ref):
    pn, _, m, k = h_ref.shape
    hr = h_ref[:, 0].reshape(pn * m, k)
    hi = h_ref[:, 1].reshape(pn * m, k)
    vr = top_ref[0, :k, :]
    vi_top = top_ref[0, k:, :]
    vi_bot = bot_ref[0]

    def times_imag(x):
        return jnp.dot(x[:, :split], vi_top, preferred_element_type=jnp.float32) + jnp.dot(
            x[:, split:], vi_bot, preferred_element_type=jnp.float32)

    real = jnp.dot(hr, vr, preferred_element_type=jnp.float32) - times_imag(hi)
    imag = times_imag(hr) + jnp.dot(hi, vr, preferred_element_type=jnp.float32)
    w = real.shape[1]
    o_ref[:, 0] = real.reshape(pn, m, w).astype(o_ref.dtype)
    o_ref[:, 1] = imag.reshape(pn, m, w).astype(o_ref.dtype)


def merge_spin(half):
    pn, _, m, n = half.shape
    return half.reshape(pn, 2, 2, m, n).transpose(0, 1, 3, 2, 4).reshape(pn, 2, m, 2 * n)


def transform(half, top, bot):
    pn, _, m, k = half.shape
    b, t_rows, w = top.shape
    split = t_rows - k
    if w % 128 != 0 or split % 128 != 0 or split <= 0:
        v = jnp.concatenate([top, bot], 1).reshape(b, 2, k, w)
        hr, hi = half[:, 0], half[:, 1]
        dims = "pmk,bkw->pmbw"
        real = jnp.einsum(dims, hr, v[:, 0], preferred_element_type=jnp.float32) - jnp.einsum(
            dims, hi, v[:, 1], preferred_element_type=jnp.float32)
        imag = jnp.einsum(dims, hr, v[:, 1], preferred_element_type=jnp.float32) + jnp.einsum(
            dims, hi, v[:, 0], preferred_element_type=jnp.float32)
        out = jnp.stack([real, imag], 1).astype(jnp.bfloat16)
        return out.reshape(pn, 2, m, b * w)
    b_rows = bot.shape[1]
    flops = 8 * pn * m * k * w * b
    bytes_accessed = 2 * (half.size + top.size + bot.size + pn * 2 * m * b * w)
    return pl.pallas_call(
        functools.partial(transform_kernel, split),
        grid=(b,),
        in_specs=[
            pl.BlockSpec((pn, 2, m, k), lambda i: (0, 0, 0, 0)),
            pl.BlockSpec((1, t_rows, w), lambda i: (i, 0, 0)),
            pl.BlockSpec((1, b_rows, w), lambda i: (i, 0, 0)),
        ],
        out_specs=pl.BlockSpec((pn, 2, m, w), lambda i: (0, 0, 0, i)),
        out_shape=jax.ShapeDtypeStruct((pn, 2, m, b * w), jnp.bfloat16),
        cost_estimate=pl.CostEstimate(flops=flops, bytes_accessed=bytes_accessed, transcendentals=0),
    )(half, top, bot)


def pair_terms(batch_rows, column_rows):
    left = jnp.concatenate([batch_rows[:, :, 0, :], batch_rows[:, :, 1, :]], 0)
    real_right = jnp.concatenate([column_rows[:, :, 0, :], -column_rows[:, :, 1, :]], 0)
    imag_right = jnp.concatenate([column_rows[:, :, 1, :], column_rows[:, :, 0, :]], 0)
    right = jnp.stack([real_right, imag_right], 1)
    return jnp.einsum("pjb,pcia->bcija", left, right, preferred_element_type=jnp.float32)


def gather_group(x, axes, sizes):
    n = 1
    for size in sizes:
        n *= size
    if n > 16:
        return lax.all_gather(x, axes, axis=0)
    me = lax.axis_index(axes[0])
    for name, size in zip(axes[1:], sizes[1:]):
        me = me * size + lax.axis_index(name)
    blocks = [x]
    for shift in range(1, n):
        perm = [(i, (i + shift) % n) for i in range(n)]
        blocks.append(lax.ppermute(x, axes, perm))
    stacked = jnp.stack(blocks, 0)
    return jnp.take(stacked, (me - jnp.arange(n)) % n, axis=0)


def on_device(cholesky, occ_coef, vir_coef, occ_energy, vir_energy, batch_occ):
    vectors = cholesky.shape[0]
    orbitals = cholesky.shape[1]
    occupied = occ_coef.shape[3]
    a_width = vir_coef.shape[3]
    n_pair = lax.axis_size("pair")
    n_aux = lax.axis_size("aux")
    n_parts = lax.axis_size("parts")
    rows = 4 * orbitals
    virtuals = n_pair * a_width
    b_width = virtuals // n_aux
    per_b = b_width // a_width
    batch = batch_occ.shape[0]

    n_q = n_parts * n_aux
    unit = 16 * n_q
    top_rows = rows - (rows * 3 // 13) // unit * unit
    occ_left = jnp.concatenate([occ_coef[0], -occ_coef[1]], 0)
    v_local = vir_coef.reshape(rows, a_width)

    occ_sel = jnp.take(occ_left, batch_occ, axis=2)
    half_sel = jnp.einsum(
        "kmi,pmn->pikn", occ_sel, cholesky, preferred_element_type=jnp.float32
    ).astype(jnp.bfloat16)
    by_pair = gather_group(half_sel, ("pair",), (n_pair,))
    gathered = gather_group(by_pair, ("aux",), (n_aux,))
    count = n_aux * n_pair * vectors
    half_rows = gathered.reshape(count * batch, 4, orbitals).transpose(1, 0, 2)
    sel_own = transform(merge_spin(half_rows[None]), v_local[None, :top_rows], v_local[None, top_rows:])
    sel_own = sel_own.reshape(2, count, batch, a_width)

    rows_q = top_rows // n_q
    q = lax.axis_index("parts") * n_aux + lax.axis_index("aux")
    piece = lax.dynamic_slice_in_dim(v_local, q * rows_q, rows_q, 0)
    top = lax.all_gather(piece, ("pair", "parts", "aux"), axis=0, tiled=True)
    top = top.reshape(n_pair, top_rows, a_width)
    bot = gather_group(v_local[top_rows:], ("pair",), (n_pair,))
    half = jnp.einsum(
        "kmj,pmn->pkjn", occ_left, cholesky, preferred_element_type=jnp.float32
    ).astype(jnp.bfloat16)
    pair_vectors = transform(merge_spin(half), top, bot).transpose(0, 2, 1, 3)

    sel_a = sel_own.transpose(1, 2, 0, 3)
    if n_aux == n_pair:
        perm = [(a * n_pair + z, z * n_pair + a) for a in range(n_aux) for z in range(n_pair)]
        sel_b = lax.ppermute(sel_a, ("aux", "pair"), perm)
    else:
        sel_all = lax.all_gather(sel_a, "pair", axis=0)
        sel_b = lax.dynamic_slice_in_dim(sel_all, lax.axis_index("aux") * per_b, per_b, 0)
        sel_b = sel_b.transpose(1, 2, 3, 0, 4).reshape(count, batch, 2, b_width)
    coulomb = pair_terms(sel_b, sel_a)
    paired = coulomb - jnp.swapaxes(coulomb, 2, 3)

    a_start = lax.axis_index("pair") * a_width
    b_start = lax.axis_index("aux") * b_width
    occ_e = jnp.take(occ_energy, batch_occ)
    vir_first = lax.dynamic_slice_in_dim(vir_energy, a_start, a_width)
    vir_second = lax.dynamic_slice_in_dim(vir_energy, b_start, b_width)
    denominator = (
        (occ_e[:, None] + occ_e[None, :])[None, None, :, :, None]
        - vir_first[None, None, None, None, :]
        - vir_second[:, None, None, None, None]
    )
    amplitudes = paired / denominator
    return (pair_vectors, amplitudes)


def solution(mesh):
    return jax.shard_map(
        on_device,
        mesh=mesh,
        in_specs=(
            P(("parts", "aux", "pair"), None, None),
            P(),
            P(None, None, None, "pair"),
            P(),
            P(),
            P(),
        ),
        out_specs=(
            P(("parts", "aux", "pair"), None, None, None),
            P(("parts", "aux"), None, None, None, "pair"),
        ),
        check_vma=False,
    )
```

```python
import functools

import jax
import jax.numpy as jnp
from jax import lax
from jax.experimental import pallas as pl
from jax.experimental.pallas import tpu as pltpu
from jax.sharding import PartitionSpec as P


def transform_kernel(orbitals, h_ref, v_ref, o_ref):
    pn, _, m, n = h_ref.shape
    per = orbitals // v_ref.shape[2]

    def rows_of(t):
        return jnp.concatenate([v_ref[t * per + j, 0] for j in range(per)], 0)

    real = None
    imag = None
    for s in range(2):
        hr = h_ref[:, s].reshape(pn * m, n)
        hi = h_ref[:, 2 + s].reshape(pn * m, n)
        vr = rows_of(s)
        vi = rows_of(2 + s)
        rr = jnp.dot(hr, vr, preferred_element_type=jnp.float32)
        ii = jnp.dot(hi, vi, preferred_element_type=jnp.float32)
        ri = jnp.dot(hr, vi, preferred_element_type=jnp.float32)
        ir = jnp.dot(hi, vr, preferred_element_type=jnp.float32)
        real = rr - ii if real is None else real + rr - ii
        imag = ri + ir if imag is None else imag + ri + ir
    w = real.shape[1]
    o_ref[:, 0] = real.reshape(pn, m, w).astype(o_ref.dtype)
    o_ref[:, 1] = imag.reshape(pn, m, w).astype(o_ref.dtype)


def transform(half, pieces):
    pn, _, m, n = half.shape
    q, b, r, w = pieces.shape
    if w % 128 != 0 or n % r != 0:
        v = pieces.transpose(1, 0, 2, 3).reshape(b, 2, 2, n, w)
        hr, hi = half[:, :2], half[:, 2:]
        dims = "pskn,bsnw->pkbw"
        real = jnp.einsum(dims, hr, v[:, 0], preferred_element_type=jnp.float32) - jnp.einsum(
            dims, hi, v[:, 1], preferred_element_type=jnp.float32)
        imag = jnp.einsum(dims, hr, v[:, 1], preferred_element_type=jnp.float32) + jnp.einsum(
            dims, hi, v[:, 0], preferred_element_type=jnp.float32)
        out = jnp.stack([real, imag], 1).astype(jnp.bfloat16)
        return out.reshape(pn, 2, m, b * w)
    flops = 16 * pn * m * n * w * b
    bytes_accessed = 2 * (half.size + pieces.size + pn * 2 * m * b * w)
    return pl.pallas_call(
        functools.partial(transform_kernel, n),
        grid=(b,),
        in_specs=[
            pl.BlockSpec((pn, 4, m, n), lambda i: (0, 0, 0, 0)),
            pl.BlockSpec((q, 1, r, w), lambda i: (0, i, 0, 0)),
        ],
        out_specs=pl.BlockSpec((pn, 2, m, w), lambda i: (0, 0, 0, i)),
        out_shape=jax.ShapeDtypeStruct((pn, 2, m, b * w), jnp.bfloat16),
        cost_estimate=pl.CostEstimate(flops=flops, bytes_accessed=bytes_accessed, transcendentals=0),
    )(half, pieces)


def pair_terms(batch_rows, column_rows):
    left = jnp.concatenate([batch_rows[:, :, 0, :], batch_rows[:, :, 1, :]], 0)
    real_right = jnp.concatenate([column_rows[:, :, 0, :], -column_rows[:, :, 1, :]], 0)
    imag_right = jnp.concatenate([column_rows[:, :, 1, :], column_rows[:, :, 0, :]], 0)
    right = jnp.stack([real_right, imag_right], 1)
    return jnp.einsum("pjb,pcia->bcija", left, right, preferred_element_type=jnp.float32)


def gather_group(x, axes, sizes):
    n = 1
    for size in sizes:
        n *= size
    if n > 16:
        return lax.all_gather(x, axes, axis=0)
    me = lax.axis_index(axes[0])
    for name, size in zip(axes[1:], sizes[1:]):
        me = me * size + lax.axis_index(name)
    blocks = [x]
    for shift in range(1, n):
        perm = [(i, (i + shift) % n) for i in range(n)]
        blocks.append(lax.ppermute(x, axes, perm))
    stacked = jnp.stack(blocks, 0)
    return jnp.take(stacked, (me - jnp.arange(n)) % n, axis=0)


def on_device(cholesky, occ_coef, vir_coef, occ_energy, vir_energy, batch_occ):
    vectors = cholesky.shape[0]
    orbitals = cholesky.shape[1]
    occupied = occ_coef.shape[3]
    a_width = vir_coef.shape[3]
    n_pair = lax.axis_size("pair")
    n_aux = lax.axis_size("aux")
    n_parts = lax.axis_size("parts")
    rows = 4 * orbitals
    virtuals = n_pair * a_width
    b_width = virtuals // n_aux
    per_b = b_width // a_width
    batch = batch_occ.shape[0]

    occ_left = jnp.concatenate([occ_coef[0], -occ_coef[1]], 0)
    v_local = vir_coef.reshape(rows, a_width)

    occ_sel = jnp.take(occ_left, batch_occ, axis=2)
    half_sel = jnp.einsum(
        "kmi,pmn->pikn", occ_sel, cholesky, preferred_element_type=jnp.float32
    ).astype(jnp.bfloat16)
    by_pair = gather_group(half_sel, ("pair",), (n_pair,))
    gathered = gather_group(by_pair, ("aux",), (n_aux,))
    count = n_aux * n_pair * vectors
    half_rows = gathered.reshape(count * batch, 4, orbitals).transpose(1, 0, 2)
    sel_own = transform(half_rows[None], v_local.reshape(8, 1, rows // 8, a_width))
    sel_own = sel_own.reshape(2, count, batch, a_width)

    n_q = n_parts * n_aux
    rows_q = rows // n_q
    q = lax.axis_index("parts") * n_aux + lax.axis_index("aux")
    piece = lax.dynamic_slice_in_dim(v_local, q * rows_q, rows_q, 0)
    v_full = lax.all_gather(piece, ("parts", "aux", "pair"), axis=0)
    v_full = v_full.reshape(n_q, n_pair, rows_q, a_width)
    half = jnp.einsum(
        "kmj,pmn->pkjn", occ_left, cholesky, preferred_element_type=jnp.float32
    ).astype(jnp.bfloat16)
    pair_vectors = transform(half, v_full).transpose(0, 2, 1, 3)

    sel_a = sel_own.transpose(1, 2, 0, 3)
    if n_aux == n_pair:
        perm = [(a * n_pair + z, z * n_pair + a) for a in range(n_aux) for z in range(n_pair)]
        sel_b = lax.ppermute(sel_a, ("aux", "pair"), perm)
    else:
        sel_all = lax.all_gather(sel_a, "pair", axis=0)
        sel_b = lax.dynamic_slice_in_dim(sel_all, lax.axis_index("aux") * per_b, per_b, 0)
        sel_b = sel_b.transpose(1, 2, 3, 0, 4).reshape(count, batch, 2, b_width)
    coulomb = pair_terms(sel_b, sel_a)
    paired = coulomb - jnp.swapaxes(coulomb, 2, 3)

    a_start = lax.axis_index("pair") * a_width
    b_start = lax.axis_index("aux") * b_width
    occ_e = jnp.take(occ_energy, batch_occ)
    vir_first = lax.dynamic_slice_in_dim(vir_energy, a_start, a_width)
    vir_second = lax.dynamic_slice_in_dim(vir_energy, b_start, b_width)
    denominator = (
        (occ_e[:, None] + occ_e[None, :])[None, None, :, :, None]
        - vir_first[None, None, None, None, :]
        - vir_second[:, None, None, None, None]
    )
    amplitudes = paired / denominator
    return (pair_vectors, amplitudes)


def solution(mesh):
    return jax.shard_map(
        on_device,
        mesh=mesh,
        in_specs=(
            P(("parts", "aux", "pair"), None, None),
            P(),
            P(None, None, None, "pair"),
            P(),
            P(),
            P(),
        ),
        out_specs=(
            P(("parts", "aux", "pair"), None, None, None),
            P(("parts", "aux"), None, None, None, "pair"),
        ),
        check_vma=False,
    )
```

```python
import functools

import jax
import jax.numpy as jnp
from jax import lax
from jax.experimental import pallas as pl
from jax.experimental.pallas import tpu as pltpu
from jax.sharding import PartitionSpec as P


def transform_kernel(h_ref, v_ref, o_ref):
    pn, _, m, k = h_ref.shape
    half_q = v_ref.shape[0] // 2
    vr = jnp.concatenate([v_ref[j, 0] for j in range(half_q)], 0)
    vi = jnp.concatenate([v_ref[half_q + j, 0] for j in range(half_q)], 0)
    hr = h_ref[:, 0].reshape(pn * m, k)
    hi = h_ref[:, 1].reshape(pn * m, k)
    real = jnp.dot(hr, vr, preferred_element_type=jnp.float32) - jnp.dot(
        hi, vi, preferred_element_type=jnp.float32)
    imag = jnp.dot(hr, vi, preferred_element_type=jnp.float32) + jnp.dot(
        hi, vr, preferred_element_type=jnp.float32)
    w = real.shape[1]
    o_ref[:, 0] = real.reshape(pn, m, w).astype(o_ref.dtype)
    o_ref[:, 1] = imag.reshape(pn, m, w).astype(o_ref.dtype)


def merge_spin(half):
    pn, _, m, n = half.shape
    return half.reshape(pn, 2, 2, m, n).transpose(0, 1, 3, 2, 4).reshape(pn, 2, m, 2 * n)


def transform(half, pieces):
    pn, _, m, k = half.shape
    q, b, r, w = pieces.shape
    if w % 128 != 0 or q % 2 != 0 or (q // 2) * r != k:
        v = pieces.transpose(1, 0, 2, 3).reshape(b, 2, k, w)
        hr, hi = half[:, 0], half[:, 1]
        dims = "pmk,bkw->pmbw"
        real = jnp.einsum(dims, hr, v[:, 0], preferred_element_type=jnp.float32) - jnp.einsum(
            dims, hi, v[:, 1], preferred_element_type=jnp.float32)
        imag = jnp.einsum(dims, hr, v[:, 1], preferred_element_type=jnp.float32) + jnp.einsum(
            dims, hi, v[:, 0], preferred_element_type=jnp.float32)
        out = jnp.stack([real, imag], 1).astype(jnp.bfloat16)
        return out.reshape(pn, 2, m, b * w)
    flops = 8 * pn * m * k * w * b
    bytes_accessed = 2 * (half.size + pieces.size + pn * 2 * m * b * w)
    return pl.pallas_call(
        transform_kernel,
        grid=(b,),
        in_specs=[
            pl.BlockSpec((pn, 2, m, k), lambda i: (0, 0, 0, 0)),
            pl.BlockSpec((q, 1, r, w), lambda i: (0, i, 0, 0)),
        ],
        out_specs=pl.BlockSpec((pn, 2, m, w), lambda i: (0, 0, 0, i)),
        out_shape=jax.ShapeDtypeStruct((pn, 2, m, b * w), jnp.bfloat16),
        cost_estimate=pl.CostEstimate(flops=flops, bytes_accessed=bytes_accessed, transcendentals=0),
    )(half, pieces)


def pair_terms(batch_rows, column_rows):
    left = jnp.concatenate([batch_rows[:, :, 0, :], batch_rows[:, :, 1, :]], 0)
    real_right = jnp.concatenate([column_rows[:, :, 0, :], -column_rows[:, :, 1, :]], 0)
    imag_right = jnp.concatenate([column_rows[:, :, 1, :], column_rows[:, :, 0, :]], 0)
    right = jnp.stack([real_right, imag_right], 1)
    return jnp.einsum("pjb,pcia->bcija", left, right, preferred_element_type=jnp.float32)


def gather_group(x, axes, sizes):
    n = 1
    for size in sizes:
        n *= size
    if n > 16:
        return lax.all_gather(x, axes, axis=0)
    me = lax.axis_index(axes[0])
    for name, size in zip(axes[1:], sizes[1:]):
        me = me * size + lax.axis_index(name)
    blocks = [x]
    for shift in range(1, n):
        perm = [(i, (i + shift) % n) for i in range(n)]
        blocks.append(lax.ppermute(x, axes, perm))
    stacked = jnp.stack(blocks, 0)
    return jnp.take(stacked, (me - jnp.arange(n)) % n, axis=0)


def on_device(cholesky, occ_coef, vir_coef, occ_energy, vir_energy, batch_occ):
    vectors = cholesky.shape[0]
    orbitals = cholesky.shape[1]
    occupied = occ_coef.shape[3]
    a_width = vir_coef.shape[3]
    n_pair = lax.axis_size("pair")
    n_aux = lax.axis_size("aux")
    n_parts = lax.axis_size("parts")
    rows = 4 * orbitals
    virtuals = n_pair * a_width
    b_width = virtuals // n_aux
    per_b = b_width // a_width
    batch = batch_occ.shape[0]

    occ_left = jnp.concatenate([occ_coef[0], -occ_coef[1]], 0)
    v_local = vir_coef.reshape(rows, a_width)

    occ_sel = jnp.take(occ_left, batch_occ, axis=2)
    half_sel = jnp.einsum(
        "kmi,pmn->pikn", occ_sel, cholesky, preferred_element_type=jnp.float32
    ).astype(jnp.bfloat16)
    by_pair = gather_group(half_sel, ("pair",), (n_pair,))
    gathered = gather_group(by_pair, ("aux",), (n_aux,))
    count = n_aux * n_pair * vectors
    half_rows = gathered.reshape(count * batch, 4, orbitals).transpose(1, 0, 2)
    sel_own = transform(merge_spin(half_rows[None]), v_local.reshape(8, 1, rows // 8, a_width))
    sel_own = sel_own.reshape(2, count, batch, a_width)

    n_q = n_parts * n_aux
    rows_q = rows // n_q
    q = lax.axis_index("parts") * n_aux + lax.axis_index("aux")
    piece = lax.dynamic_slice_in_dim(v_local, q * rows_q, rows_q, 0)
    v_full = lax.all_gather(piece, ("parts", "aux", "pair"), axis=0)
    v_full = v_full.reshape(n_q, n_pair, rows_q, a_width)
    half = jnp.einsum(
        "kmj,pmn->pkjn", occ_left, cholesky, preferred_element_type=jnp.float32
    ).astype(jnp.bfloat16)
    pair_vectors = transform(merge_spin(half), v_full).transpose(0, 2, 1, 3)

    sel_a = sel_own.transpose(1, 2, 0, 3)
    if n_aux == n_pair:
        perm = [(a * n_pair + z, z * n_pair + a) for a in range(n_aux) for z in range(n_pair)]
        sel_b = lax.ppermute(sel_a, ("aux", "pair"), perm)
    else:
        sel_all = lax.all_gather(sel_a, "pair", axis=0)
        sel_b = lax.dynamic_slice_in_dim(sel_all, lax.axis_index("aux") * per_b, per_b, 0)
        sel_b = sel_b.transpose(1, 2, 3, 0, 4).reshape(count, batch, 2, b_width)
    coulomb = pair_terms(sel_b, sel_a)
    paired = coulomb - jnp.swapaxes(coulomb, 2, 3)

    a_start = lax.axis_index("pair") * a_width
    b_start = lax.axis_index("aux") * b_width
    occ_e = jnp.take(occ_energy, batch_occ)
    vir_first = lax.dynamic_slice_in_dim(vir_energy, a_start, a_width)
    vir_second = lax.dynamic_slice_in_dim(vir_energy, b_start, b_width)
    denominator = (
        (occ_e[:, None] + occ_e[None, :])[None, None, :, :, None]
        - vir_first[None, None, None, None, :]
        - vir_second[:, None, None, None, None]
    )
    amplitudes = paired / denominator
    return (pair_vectors, amplitudes)


def solution(mesh):
    return jax.shard_map(
        on_device,
        mesh=mesh,
        in_specs=(
            P(("parts", "aux", "pair"), None, None),
            P(),
            P(None, None, None, "pair"),
            P(),
            P(),
            P(),
        ),
        out_specs=(
            P(("parts", "aux", "pair"), None, None, None),
            P(("parts", "aux"), None, None, None, "pair"),
        ),
        check_vma=False,
    )
```
